32 devices in a mesh: row: 8 (over y, x, core), col: 4 (over z).
Axes of the slice: x: 2, y: 2, z: 4, core: 2. Of those that a mesh axis runs over, the one named last changes fastest.
Arguments:
- left_values: bfloat16 [8, 4, 64, 128, 128], P('row', 'col'), may hold values from -6 to 6
- left_places: int32 [8, 4, 64], replicated, may hold values from 0 to 127, as said below
- right_values: bfloat16 [8, 4, 64, 128, 128], P('row', 'col'), may hold values from -0.25 to 0.25
- right_places: int32 [8, 4, 64], replicated, may hold values from 0 to 255, as said below
- owners: int32 [32, 128], P(('row', 'col')), may hold values from 0 to 31, as said below
Outputs:
- inbox: bfloat16 [32, 32, 8, 128, 128], P(('row', 'col'))
The draws below stay inside these ranges and needn't reach their ends.
Inputs may be any that keep to these rules, and one draw needn't show every extreme that they name: `left_places`: within one tile's list the 64 positions are distinct. `right_places`: within one tile's list the 64 positions are distinct. Each row of owners names each device at most 8 times; in every draw some device is named exactly 8 times by every row.
All inputs are finite; a program needn't handle non-finite values.
Results may differ from the reference program's by a relative error of at most 0.001.
Values may be sent and summed in bfloat16 or wider, within the bound.
No kernel may reach another device: no remote copies, remote signals or barrier semaphores. Data moves between devices by JAX's collectives and lax.ppermute only.
A program may use at most 256 MiB of HBM per device.

```python
import jax
import jax.numpy as jnp
from jax import lax

BLOCK = 128
ROWB = 8
KBLK = 16
COLB = 16
A_BLOCKS = 64
B_BLOCKS = 64
PRODUCTS = 128
CAP = 8
N_ROW = 8
N_COL = 4
DEVICES = 32


def draw_tile_lists(key, positions, count):
    keys = jax.random.split(key, N_ROW * N_COL)

    def one_tile(subkey):
        return jax.random.permutation(subkey, positions)[:count]
    lists = jax.vmap(one_tile)(keys)
    return lists.reshape(N_ROW, N_COL, count).astype(jnp.int32)


def draw_left_places(key, part):
    return draw_tile_lists(jax.random.fold_in(key, 3), ROWB * KBLK, A_BLOCKS)


def draw_right_places(key, part):
    return draw_tile_lists(jax.random.fold_in(key, 5), KBLK * COLB, B_BLOCKS)


def draw_owners(key, part):
    hot_owner = jax.random.randint(jax.random.fold_in(key, 7), (), 0, DEVICES).astype(jnp.int32)
    keys = jax.random.split(jax.random.fold_in(key, 11), DEVICES)

    def one_source(subkey):
        first_key, second_key = jax.random.split(subkey)
        spread = jax.random.permutation(first_key, CAP * (DEVICES - 1))[:PRODUCTS - CAP].astype(jnp.int32)
        others = (hot_owner + 1 + spread // CAP) % DEVICES
        listed = jnp.concatenate([jnp.full((CAP,), hot_owner, jnp.int32), others.astype(jnp.int32)])
        return jax.random.permutation(second_key, listed)
    return jax.vmap(one_source)(keys).astype(jnp.int32)


def shard_levels(stream_key, dims, pieces, smallest, largest):
    level, own = 1.0, jax.random.fold_in(stream_key, 6)
    for position, parts in pieces:
        steps = jnp.exp(jax.random.uniform(jax.random.fold_in(own, position), (parts,), jnp.float32, smallest / len(pieces), largest / len(pieces)))
        level = level * jnp.repeat(steps, dims[position] // parts).reshape([-1 if axis == position else 1 for axis in range(len(dims))])
    return level


def normal_values(own_key, shape, scale, limit, shards=(), held_as=jnp.bfloat16):
    values = scale * jax.random.normal(own_key, shape, jnp.float32)
    if shards:
        values = values * shard_levels(own_key, shape, shards, -0.22, 0.18)
    return jnp.clip(values, -limit, limit).astype(held_as)


def setup_inputs(seed: int = 0) -> dict:
    splits = jax.random.split(jax.random.key(seed), 6)
    left_values = normal_values(splits[0], (N_ROW, N_COL, A_BLOCKS, BLOCK, BLOCK), 1.0, 6.0, ((0, 8), (1, 4)))
    left_places = draw_left_places(jax.random.fold_in(splits[5], 71), 0)
    right_values = normal_values(splits[2], (N_ROW, N_COL, B_BLOCKS, BLOCK, BLOCK), (BLOCK * KBLK // 4) ** -0.5, 0.25, ((0, 8), (1, 4)))
    right_places = draw_right_places(jax.random.fold_in(splits[5], 71), 0)
    owners = draw_owners(jax.random.fold_in(splits[5], 71), 0)
    return {"left_values": left_values, "left_places": left_places, "right_values": right_values, "right_places": right_places, "owners": owners}


def densify(values, places, row_count, col_count):
    side_len = values.shape[-1]
    stacked = jnp.zeros((row_count * col_count, side_len, side_len), values.dtype)
    stacked = stacked.at[places.astype(jnp.int32)].set(values)
    stacked = stacked.reshape(row_count, col_count, side_len, side_len).transpose(0, 2, 1, 3)
    return stacked.reshape(row_count * side_len, col_count * side_len)


def reference(left_values, left_places, right_values, right_places, owners):
    side_len = left_values.shape[-1]

    def one_source(source):
        row_here = source // N_COL
        col_here = source % N_COL
        row_next = (row_here + 1) % N_ROW
        col_next = (col_here + 1) % N_COL
        left_first = densify(left_values[row_here, col_here], left_places[row_here, col_here], ROWB, KBLK)
        right_first = densify(right_values[row_here, col_here], right_places[row_here, col_here], KBLK, COLB)
        left_second = densify(left_values[row_here, col_next], left_places[row_here, col_next], ROWB, KBLK)
        right_second = densify(right_values[row_next, col_here], right_places[row_next, col_here], KBLK, COLB)
        product = jnp.dot(left_first, right_first, preferred_element_type=jnp.float32)
        product = product + jnp.dot(left_second, right_second, preferred_element_type=jnp.float32)
        blocks = product.astype(jnp.bfloat16).reshape(ROWB, side_len, COLB, side_len)
        blocks = blocks.transpose(0, 2, 1, 3).reshape(ROWB * COLB, side_len, side_len)
        owner_list = owners[source].astype(jnp.int32)
        positions = jnp.arange(ROWB * COLB, dtype=jnp.int32)
        same_owner = owner_list[None, :] == owner_list[:, None]
        earlier = positions[None, :] < positions[:, None]
        slot_index = jnp.sum((same_owner & earlier).astype(jnp.int32), axis=1).astype(jnp.int32)
        outgoing = jnp.zeros((DEVICES * CAP, side_len, side_len), jnp.bfloat16)
        outgoing = outgoing.at[(owner_list * CAP + slot_index).astype(jnp.int32)].set(blocks)
        return outgoing.reshape(DEVICES, CAP, side_len, side_len)

    sent = lax.map(one_source, jnp.arange(DEVICES, dtype=jnp.int32))
    return jnp.transpose(sent, (1, 0, 2, 3, 4))
```

```python
import jax
import jax.numpy as jnp
from jax import lax
from jax.sharding import PartitionSpec as P

ROWB = 8
KBLK = 16
COLB = 16


def from_behind(block, axis, distance):
    devices = range(lax.axis_size(axis))
    route = [((i - distance) % len(devices), i) for i in devices]
    return lax.ppermute(block, axis, route)


def dense_blocks(values, places, row_count, col_count):
    count = values.shape[0]
    positions = row_count * col_count
    index = jnp.full((positions,), count, jnp.int32).at[places].set(
        jnp.arange(count, dtype=jnp.int32)
    )
    present = index < count
    taken = values[jnp.minimum(index, count - 1)]
    taken = jnp.where(present[:, None, None], taken, jnp.zeros_like(taken))
    side_len = values.shape[-1]
    return taken.reshape(row_count, col_count, side_len, side_len)


def term(left_blocks, right_blocks):
    return jnp.einsum(
        "rkab,kcbd->rcad", left_blocks, right_blocks, preferred_element_type=jnp.float32
    )


def body(left_values, left_places, right_values, right_places, owners):
    rows_grid = lax.axis_size("row")
    cols_grid = lax.axis_size("col")
    devices_all = rows_grid * cols_grid
    row_here = lax.axis_index("row")
    col_here = lax.axis_index("col")
    row_next = (row_here + 1) % rows_grid
    col_next = (col_here + 1) % cols_grid
    left_here = left_values[0, 0]
    right_here = right_values[0, 0]
    side_len = left_here.shape[-1]
    left_next = from_behind(left_here, "col", -1)
    right_next = from_behind(right_here, "row", -1)
    left_first = dense_blocks(left_here, left_places[row_here, col_here], ROWB, KBLK)
    right_first = dense_blocks(right_here, right_places[row_here, col_here], KBLK, COLB)
    left_second = dense_blocks(left_next, left_places[row_here, col_next], ROWB, KBLK)
    right_second = dense_blocks(right_next, right_places[row_next, col_here], KBLK, COLB)
    product = term(left_first, right_first) + term(left_second, right_second)
    blocks = product.astype(jnp.bfloat16).reshape(ROWB * COLB, side_len, side_len)
    capacity = 2 * ROWB * COLB // devices_all
    owner_list = owners[0]
    product_count = ROWB * COLB
    positions = jnp.arange(product_count, dtype=jnp.int32)
    same_owner = owner_list[None, :] == owner_list[:, None]
    earlier = positions[None, :] < positions[:, None]
    slot_index = jnp.sum((same_owner & earlier).astype(jnp.int32), axis=1)
    slots = devices_all * capacity
    source_of = jnp.full((slots,), product_count, jnp.int32).at[
        owner_list * capacity + slot_index
    ].set(positions)
    filled = source_of < product_count
    outgoing = blocks[jnp.minimum(source_of, product_count - 1)]
    outgoing = jnp.where(filled[:, None, None], outgoing, jnp.zeros_like(outgoing))
    outgoing = outgoing.reshape(devices_all, capacity, side_len, side_len)
    received = lax.all_to_all(outgoing, ("row", "col"), split_axis=0, concat_axis=0, tiled=True)
    return received[None]


def solution(mesh):
    placed = (
        P("row", "col", None, None, None),
        P(),
        P("row", "col", None, None, None),
        P(),
        P(("row", "col"), None),
    )
    return jax.shard_map(
        body,
        mesh=mesh,
        in_specs=placed,
        out_specs=P(("row", "col"), None, None, None, None),
        check_vma=False,
    )
```

```python
import functools

import jax
import jax.numpy as jnp
from jax import lax
from jax.experimental import pallas as pl
from jax.experimental.pallas import tpu as pltpu
from jax.sharding import PartitionSpec as P

ROWB = 8
KBLK = 16
COLB = 16
COL_GROUP = 2
ROW_GROUP = 2


def from_behind(block, axis, distance):
    devices = range(lax.axis_size(axis))
    route = [((i - distance) % len(devices), i) for i in devices]
    return lax.ppermute(block, axis, route)


def product_kernel(
    rows_grid, cols_grid, capacity,
    left_places, right_places, owners,
    left_first, left_second, right_first, right_second,
    out,
    left_dense, right_column, left_index, right_index, slot_of, filled, counts,
):
    side = left_first.shape[-1]
    stored = left_first.shape[0]
    row_here = lax.axis_index("row")
    col_here = lax.axis_index("col")
    row_next = lax.rem(row_here + 1, rows_grid)
    col_next = lax.rem(col_here + 1, cols_grid)
    tile_len = left_places.shape[0] // (rows_grid * cols_grid)
    left_bases = ((row_here * cols_grid + col_here) * tile_len, (row_here * cols_grid + col_next) * tile_len)
    right_bases = ((row_here * cols_grid + col_here) * tile_len, (row_next * cols_grid + col_here) * tile_len)
    left_positions = ROWB * KBLK
    right_positions = KBLK * COLB
    slots = out.shape[0]
    products = ROWB * COLB

    def clear_left(p, carry):
        left_index[p] = -1
        return carry

    lax.fori_loop(0, 2 * left_positions, clear_left, 0)

    def clear_right(p, carry):
        right_index[p] = -1
        return carry

    lax.fori_loop(0, 2 * right_positions, clear_right, 0)

    def clear_slots(s, carry):
        filled[s] = 0
        return carry

    lax.fori_loop(0, slots, clear_slots, 0)

    def clear_counts(d, carry):
        counts[d] = 0
        return carry

    lax.fori_loop(0, counts.shape[0], clear_counts, 0)

    def invert(n, carry):
        for t in range(2):
            left_index[t * left_positions + left_places[left_bases[t] + n]] = n
            right_index[t * right_positions + right_places[right_bases[t] + n]] = n
        return carry

    lax.fori_loop(0, stored, invert, 0)

    def assign(m, carry):
        owner = owners[m]
        taken = counts[owner]
        slot = owner * capacity + taken
        slot_of[m] = slot
        filled[slot] = 1
        counts[owner] = taken + 1
        return carry

    lax.fori_loop(0, products, assign, 0)

    left_tiles = (left_first, left_second)
    right_tiles = (right_first, right_second)
    zero_block = jnp.zeros((side, side), left_first.dtype)

    def densify_left(r, carry):
        rows = pl.ds(pl.multiple_of(r * side, side), side)
        for t in range(2):
            for k in range(KBLK):
                index = left_index[t * left_positions + r * KBLK + k]
                block = left_tiles[t][jnp.maximum(index, 0)]
                column = (t * KBLK + k) * side
                left_dense[rows, column:column + side] = jnp.where(index >= 0, block, zero_block)
        return carry

    lax.fori_loop(0, ROWB, densify_left, 0)

    def column_pair(cp, carry):
        for t in range(2):
            for k in range(KBLK):
                for cc in range(COL_GROUP):
                    index = right_index[t * right_positions + k * COLB + cp * COL_GROUP + cc]
                    block = right_tiles[t][jnp.maximum(index, 0)]
                    row = (t * KBLK + k) * side
                    right_column[row:row + side, cc * side:(cc + 1) * side] = jnp.where(
                        index >= 0, block, zero_block
                    )

        def row_pair(rp, inner):
            rows = pl.ds(pl.multiple_of(rp * ROW_GROUP * side, ROW_GROUP * side), ROW_GROUP * side)
            result = jnp.dot(left_dense[rows, :], right_column[...], preferred_element_type=jnp.float32)
            for rr in range(ROW_GROUP):
                for cc in range(COL_GROUP):
                    m = (rp * ROW_GROUP + rr) * COLB + cp * COL_GROUP + cc
                    piece = result[rr * side:(rr + 1) * side, cc * side:(cc + 1) * side]
                    out[slot_of[m]] = piece.astype(out.dtype)
            return inner

        lax.fori_loop(0, ROWB // ROW_GROUP, row_pair, 0)
        return carry

    lax.fori_loop(0, COLB // COL_GROUP, column_pair, 0)

    def zero_slot(s, carry):
        @pl.when(filled[s] == 0)
        def _():
            out[s] = zero_block

        return carry

    lax.fori_loop(0, slots, zero_slot, 0)


def body(left_values, left_places, right_values, right_places, owners):
    rows_grid = lax.axis_size("row")
    cols_grid = lax.axis_size("col")
    devices_all = rows_grid * cols_grid
    left_here = left_values[0, 0]
    right_here = right_values[0, 0]
    side = left_here.shape[-1]
    left_next = from_behind(left_here, "col", -1)
    right_next = from_behind(right_here, "row", -1)
    capacity = 2 * ROWB * COLB // devices_all
    slots = devices_all * capacity
    smem = pl.BlockSpec(memory_space=pltpu.SMEM)
    vmem = pl.BlockSpec(memory_space=pltpu.VMEM)
    kernel = functools.partial(product_kernel, rows_grid, cols_grid, capacity)
    flops = 2 * (ROWB * side) * (2 * KBLK * side) * (COLB * side)
    outgoing = pl.pallas_call(
        kernel,
        out_shape=jax.ShapeDtypeStruct((slots, side, side), jnp.bfloat16),
        in_specs=[smem, smem, smem, vmem, vmem, vmem, vmem],
        out_specs=vmem,
        scratch_shapes=[
            pltpu.VMEM((ROWB * side, 2 * KBLK * side), jnp.bfloat16),
            pltpu.VMEM((2 * KBLK * side, COL_GROUP * side), jnp.bfloat16),
            pltpu.SMEM((2 * ROWB * KBLK,), jnp.int32),
            pltpu.SMEM((2 * KBLK * COLB,), jnp.int32),
            pltpu.SMEM((ROWB * COLB,), jnp.int32),
            pltpu.SMEM((slots,), jnp.int32),
            pltpu.SMEM((devices_all,), jnp.int32),
        ],
        compiler_params=pltpu.CompilerParams(vmem_limit_bytes=60 * 1024 * 1024),
        cost_estimate=pl.CostEstimate(
            flops=flops, bytes_accessed=4 * left_here.size * 2 + slots * side * side * 2, transcendentals=0
        ),
    )(
        left_places.reshape(-1),
        right_places.reshape(-1),
        owners[0],
        left_here,
        left_next,
        right_here,
        right_next,
    )
    outgoing = outgoing.reshape(devices_all, capacity, side, side)
    received = lax.all_to_all(outgoing, ("row", "col"), split_axis=0, concat_axis=0, tiled=True)
    return received[None]


def solution(mesh):
    placed = (
        P("row", "col", None, None, None),
        P(),
        P("row", "col", None, None, None),
        P(),
        P(("row", "col"), None),
    )
    return jax.shard_map(
        body,
        mesh=mesh,
        in_specs=placed,
        out_specs=P(("row", "col"), None, None, None, None),
        check_vma=False,
    )
```

```python
import functools

import jax
import jax.numpy as jnp
from jax import lax
from jax.experimental import pallas as pl
from jax.experimental.pallas import tpu as pltpu
from jax.sharding import PartitionSpec as P

ROWB = 8
KBLK = 16
COLB = 16
COL_GROUP = 2
ROW_GROUP = 2


def from_behind(block, axis, distance):
    devices = range(lax.axis_size(axis))
    route = [((i - distance) % len(devices), i) for i in devices]
    return lax.ppermute(block, axis, route)


def fill(ref, count, value):
    def step(i, carry):
        ref[i] = value
        return carry

    lax.fori_loop(0, count, step, 0)


def tile_bases(rows_grid, cols_grid, tile_len, second):
    row_here = lax.axis_index("row")
    col_here = lax.axis_index("col")
    if second:
        left_tile = row_here * cols_grid + lax.rem(col_here + 1, cols_grid)
        right_tile = lax.rem(row_here + 1, rows_grid) * cols_grid + col_here
    else:
        left_tile = row_here * cols_grid + col_here
        right_tile = left_tile
    return left_tile * tile_len, right_tile * tile_len


def multiply_tiles(
    rows_grid, cols_grid, left_places, right_places, left_tile, right_tile,
    left_dense, right_column, left_index, right_index, second, emit,
):
    side = left_tile.shape[-1]
    stored = left_tile.shape[0]
    tile_len = left_places.shape[0] // (rows_grid * cols_grid)
    left_base, right_base = tile_bases(rows_grid, cols_grid, tile_len, second)
    fill(left_index, ROWB * KBLK, -1)
    fill(right_index, KBLK * COLB, -1)

    def invert(n, carry):
        left_index[left_places[left_base + n]] = n
        right_index[right_places[right_base + n]] = n
        return carry

    lax.fori_loop(0, stored, invert, 0)
    zero_block = jnp.zeros((side, side), left_tile.dtype)

    def densify_left(r, carry):
        rows = pl.ds(pl.multiple_of(r * side, side), side)
        for k in range(KBLK):
            index = left_index[r * KBLK + k]
            block = left_tile[jnp.maximum(index, 0)]
            left_dense[rows, k * side:(k + 1) * side] = jnp.where(index >= 0, block, zero_block)
        return carry

    lax.fori_loop(0, ROWB, densify_left, 0)

    def column_pair(cp, carry):
        for k in range(KBLK):
            for cc in range(COL_GROUP):
                index = right_index[k * COLB + cp * COL_GROUP + cc]
                block = right_tile[jnp.maximum(index, 0)]
                right_column[k * side:(k + 1) * side, cc * side:(cc + 1) * side] = jnp.where(
                    index >= 0, block, zero_block
                )

        def row_pair(rp, inner):
            rows = pl.ds(pl.multiple_of(rp * ROW_GROUP * side, ROW_GROUP * side), ROW_GROUP * side)
            result = jnp.dot(left_dense[rows, :], right_column[...], preferred_element_type=jnp.float32)
            emit(rp, cp, rows, result)
            return inner

        lax.fori_loop(0, ROWB // ROW_GROUP, row_pair, 0)
        return carry

    lax.fori_loop(0, COLB // COL_GROUP, column_pair, 0)


def first_kernel(
    rows_grid, cols_grid, capacity,
    left_places, right_places, owners, left_tile, right_tile,
    partial, slot_of, filled,
    left_dense, right_column, left_index, right_index, counts,
):
    side = left_tile.shape[-1]
    fill(filled, filled.shape[0], 0)
    fill(counts, counts.shape[0], 0)

    def assign(m, carry):
        owner = owners[m]
        taken = counts[owner]
        slot = owner * capacity + taken
        slot_of[m] = slot
        filled[slot] = 1
        counts[owner] = taken + 1
        return carry

    lax.fori_loop(0, ROWB * COLB, assign, 0)

    def emit(rp, cp, rows, result):
        columns = pl.ds(pl.multiple_of(cp * COL_GROUP * side, COL_GROUP * side), COL_GROUP * side)
        partial[rows, columns] = result

    multiply_tiles(
        rows_grid, cols_grid, left_places, right_places, left_tile, right_tile,
        left_dense, right_column, left_index, right_index, False, emit,
    )


def second_kernel(
    rows_grid, cols_grid,
    left_places, right_places, slot_of, filled, left_tile, right_tile, partial,
    out,
    left_dense, right_column, left_index, right_index,
):
    side = left_tile.shape[-1]

    def emit(rp, cp, rows, result):
        columns = pl.ds(pl.multiple_of(cp * COL_GROUP * side, COL_GROUP * side), COL_GROUP * side)
        total = result + partial[rows, columns]
        for rr in range(ROW_GROUP):
            for cc in range(COL_GROUP):
                m = (rp * ROW_GROUP + rr) * COLB + cp * COL_GROUP + cc
                piece = total[rr * side:(rr + 1) * side, cc * side:(cc + 1) * side]
                out[slot_of[m]] = piece.astype(out.dtype)

    multiply_tiles(
        rows_grid, cols_grid, left_places, right_places, left_tile, right_tile,
        left_dense, right_column, left_index, right_index, True, emit,
    )
    zero_block = jnp.zeros((side, side), out.dtype)

    def zero_slot(s, carry):
        @pl.when(filled[s] == 0)
        def _():
            out[s] = zero_block

        return carry

    lax.fori_loop(0, out.shape[0], zero_slot, 0)


def body(left_values, left_places, right_values, right_places, owners):
    rows_grid = lax.axis_size("row")
    cols_grid = lax.axis_size("col")
    devices_all = rows_grid * cols_grid
    left_here = left_values[0, 0]
    right_here = right_values[0, 0]
    side = left_here.shape[-1]
    left_next = from_behind(left_here, "col", -1)
    right_next = from_behind(right_here, "row", -1)
    capacity = 2 * ROWB * COLB // devices_all
    slots = devices_all * capacity
    products = ROWB * COLB
    smem = pl.BlockSpec(memory_space=pltpu.SMEM)
    vmem = pl.BlockSpec(memory_space=pltpu.VMEM)
    left_flat = left_places.reshape(-1)
    right_flat = right_places.reshape(-1)
    work = [
        pltpu.VMEM((ROWB * side, KBLK * side), jnp.bfloat16),
        pltpu.VMEM((KBLK * side, COL_GROUP * side), jnp.bfloat16),
        pltpu.SMEM((ROWB * KBLK,), jnp.int32),
        pltpu.SMEM((KBLK * COLB,), jnp.int32),
    ]
    flops = 2 * (ROWB * side) * (KBLK * side) * (COLB * side)
    tile_bytes = 2 * left_here.size * 2
    partial_bytes = ROWB * COLB * side * side * 4
    partial, slot_of, filled = pl.pallas_call(
        functools.partial(first_kernel, rows_grid, cols_grid, capacity),
        out_shape=(
            jax.ShapeDtypeStruct((ROWB * side, COLB * side), jnp.float32),
            jax.ShapeDtypeStruct((products,), jnp.int32),
            jax.ShapeDtypeStruct((slots,), jnp.int32),
        ),
        in_specs=[smem, smem, smem, vmem, vmem],
        out_specs=(vmem, smem, smem),
        scratch_shapes=work + [pltpu.SMEM((devices_all,), jnp.int32)],
        compiler_params=pltpu.CompilerParams(vmem_limit_bytes=60 * 1024 * 1024),
        cost_estimate=pl.CostEstimate(flops=flops, bytes_accessed=tile_bytes + partial_bytes, transcendentals=0),
    )(left_flat, right_flat, owners[0], left_here, right_here)
    outgoing = pl.pallas_call(
        functools.partial(second_kernel, rows_grid, cols_grid),
        out_shape=jax.ShapeDtypeStruct((slots, side, side), jnp.bfloat16),
        in_specs=[smem, smem, smem, smem, vmem, vmem, vmem],
        out_specs=vmem,
        scratch_shapes=work,
        compiler_params=pltpu.CompilerParams(vmem_limit_bytes=60 * 1024 * 1024),
        cost_estimate=pl.CostEstimate(
            flops=flops, bytes_accessed=tile_bytes + partial_bytes + slots * side * side * 2, transcendentals=0
        ),
    )(left_flat, right_flat, slot_of, filled, left_next, right_next, partial)
    outgoing = outgoing.reshape(devices_all, capacity, side, side)
    received = lax.all_to_all(outgoing, ("row", "col"), split_axis=0, concat_axis=0, tiled=True)
    return received[None]


def solution(mesh):
    placed = (
        P("row", "col", None, None, None),
        P(),
        P("row", "col", None, None, None),
        P(),
        P(("row", "col"), None),
    )
    return jax.shard_map(
        body,
        mesh=mesh,
        in_specs=placed,
        out_specs=P(("row", "col"), None, None, None, None),
        check_vma=False,
    )
```

```python
import functools

import jax
import jax.numpy as jnp
from jax import lax
from jax.experimental import pallas as pl
from jax.experimental.pallas import tpu as pltpu
from jax.sharding import PartitionSpec as P

ROWB = 8
KBLK = 16
COLB = 16
COL_GROUP = 2
ROW_GROUP = 2


def from_behind(block, axis, distance):
    devices = range(lax.axis_size(axis))
    route = [((i - distance) % len(devices), i) for i in devices]
    return lax.ppermute(block, axis, route)


def fill(ref, count, value):
    def step(i, carry):
        ref[i] = value
        return carry

    lax.fori_loop(0, count, step, 0)


def invert_places(places, base, index_ref, positions, stored):
    fill(index_ref, positions, -1)

    def step(n, carry):
        index_ref[places[base + n]] = n
        return carry

    lax.fori_loop(0, stored, step, 0)


def multiply_tiles(left_tile, right_tile, left_index, right_index, left_dense, right_column, emit, before=None):
    side = left_tile.shape[-1]
    zero_block = jnp.zeros((side, side), left_tile.dtype)

    def densify_left(r, carry):
        rows = pl.ds(pl.multiple_of(r * side, side), side)
        for k in range(KBLK):
            index = left_index[r * KBLK + k]
            block = left_tile[jnp.maximum(index, 0)]
            left_dense[rows, k * side:(k + 1) * side] = jnp.where(index >= 0, block, zero_block)
        return carry

    lax.fori_loop(0, ROWB, densify_left, 0)

    def column_pair(cp, carry):
        if before is not None:
            before(cp)
        for k in range(KBLK):
            for cc in range(COL_GROUP):
                index = right_index[k * COLB + cp * COL_GROUP + cc]
                block = right_tile[jnp.maximum(index, 0)]
                right_column[k * side:(k + 1) * side, cc * side:(cc + 1) * side] = jnp.where(
                    index >= 0, block, zero_block
                )

        def row_pair(rp, inner):
            rows = pl.ds(pl.multiple_of(rp * ROW_GROUP * side, ROW_GROUP * side), ROW_GROUP * side)
            result = jnp.dot(left_dense[rows, :], right_column[...], preferred_element_type=jnp.float32)
            emit(rp, cp, rows, result)
            return inner

        lax.fori_loop(0, ROWB // ROW_GROUP, row_pair, 0)
        return carry

    lax.fori_loop(0, COLB // COL_GROUP, column_pair, 0)


def first_kernel(
    rows_grid, cols_grid, capacity,
    left_places, right_places, owners, left_tile, right_tile,
    partial, slot_of, filled, left_index_next, right_index_next,
    left_dense, right_column, left_index, right_index, counts,
):
    side = left_tile.shape[-1]
    stored = left_tile.shape[0]
    tile_len = left_places.shape[0] // (rows_grid * cols_grid)
    row_here = lax.axis_index("row")
    col_here = lax.axis_index("col")
    tile_here = (row_here * cols_grid + col_here) * tile_len
    left_next = (row_here * cols_grid + lax.rem(col_here + 1, cols_grid)) * tile_len
    right_next = (lax.rem(row_here + 1, rows_grid) * cols_grid + col_here) * tile_len
    invert_places(left_places, tile_here, left_index, ROWB * KBLK, stored)
    invert_places(right_places, tile_here, right_index, KBLK * COLB, stored)
    invert_places(left_places, left_next, left_index_next, ROWB * KBLK, stored)
    invert_places(right_places, right_next, right_index_next, KBLK * COLB, stored)
    fill(filled, filled.shape[0], 0)
    fill(counts, counts.shape[0], 0)

    def assign(m, carry):
        owner = owners[m]
        taken = counts[owner]
        slot = owner * capacity + taken
        slot_of[m] = slot
        filled[slot] = 1
        counts[owner] = taken + 1
        return carry

    lax.fori_loop(0, ROWB * COLB, assign, 0)

    def emit(rp, cp, rows, result):
        partial[cp, rows, :] = result

    multiply_tiles(left_tile, right_tile, left_index, right_index, left_dense, right_column, emit)


def second_kernel(
    slot_of, filled, left_index, right_index, left_tile, right_tile, partial,
    out,
    left_dense, right_column, partial_buf, staging, zero_ref, partial_sems, out_sems,
):
    side = left_tile.shape[-1]
    pairs = COLB // COL_GROUP
    slots = out.shape[0]
    zero_ref[...] = jnp.zeros(zero_ref.shape, zero_ref.dtype)

    def partial_copy(cp, buffer):
        return pltpu.make_async_copy(partial.at[cp], partial_buf.at[buffer], partial_sems.at[buffer])

    partial_copy(0, 0).start()

    def zero_slot(s, carry):
        @pl.when(filled[s] == 0)
        def _():
            pltpu.make_async_copy(zero_ref, out.at[s], out_sems.at[s]).start()

        return carry

    lax.fori_loop(0, slots, zero_slot, 0)

    def send_pair(cp):
        for r in range(ROWB):
            for cc in range(COL_GROUP):
                m = r * COLB + cp * COL_GROUP + cc
                slot = slot_of[m]
                pltpu.make_async_copy(staging.at[m], out.at[slot], out_sems.at[slot]).start()

    def before(cp):
        buffer = lax.rem(cp, 2)

        @pl.when(cp + 1 < pairs)
        def _():
            partial_copy(cp + 1, 1 - buffer).start()

        @pl.when(cp > 0)
        def _():
            send_pair(cp - 1)

        partial_copy(cp, buffer).wait()

    def emit(rp, cp, rows, result):
        buffer = lax.rem(cp, 2)
        total = result + partial_buf[buffer, rows, :]
        for rr in range(ROW_GROUP):
            for cc in range(COL_GROUP):
                m = (rp * ROW_GROUP + rr) * COLB + cp * COL_GROUP + cc
                piece = total[rr * side:(rr + 1) * side, cc * side:(cc + 1) * side]
                staging[m] = piece.astype(staging.dtype)

    multiply_tiles(left_tile, right_tile, left_index, right_index, left_dense, right_column, emit, before)
    send_pair(pairs - 1)

    def wait_slot(s, carry):
        pltpu.make_async_copy(zero_ref, out.at[s], out_sems.at[s]).wait()
        return carry

    lax.fori_loop(0, slots, wait_slot, 0)


def body(left_values, left_places, right_values, right_places, owners):
    rows_grid = lax.axis_size("row")
    cols_grid = lax.axis_size("col")
    devices_all = rows_grid * cols_grid
    left_here = left_values[0, 0]
    right_here = right_values[0, 0]
    side = left_here.shape[-1]
    left_next = from_behind(left_here, "col", -1)
    right_next = from_behind(right_here, "row", -1)
    capacity = 2 * ROWB * COLB // devices_all
    slots = devices_all * capacity
    products = ROWB * COLB
    pairs = COLB // COL_GROUP
    smem = pl.BlockSpec(memory_space=pltpu.SMEM)
    vmem = pl.BlockSpec(memory_space=pltpu.VMEM)
    anywhere = pl.BlockSpec(memory_space=pl.ANY)
    left_flat = left_places.reshape(-1)
    right_flat = right_places.reshape(-1)
    work = [
        pltpu.VMEM((ROWB * side, KBLK * side), jnp.bfloat16),
        pltpu.VMEM((KBLK * side, COL_GROUP * side), jnp.bfloat16),
    ]
    flops = 2 * (ROWB * side) * (KBLK * side) * (COLB * side)
    tile_bytes = 2 * left_here.size * 2
    partial_bytes = ROWB * COLB * side * side * 4
    partial, slot_of, filled, left_index, right_index = pl.pallas_call(
        functools.partial(first_kernel, rows_grid, cols_grid, capacity),
        out_shape=(
            jax.ShapeDtypeStruct((pairs, ROWB * side, COL_GROUP * side), jnp.float32),
            jax.ShapeDtypeStruct((products,), jnp.int32),
            jax.ShapeDtypeStruct((slots,), jnp.int32),
            jax.ShapeDtypeStruct((ROWB * KBLK,), jnp.int32),
            jax.ShapeDtypeStruct((KBLK * COLB,), jnp.int32),
        ),
        in_specs=[smem, smem, smem, vmem, vmem],
        out_specs=(vmem, smem, smem, smem, smem),
        scratch_shapes=work + [
            pltpu.SMEM((ROWB * KBLK,), jnp.int32),
            pltpu.SMEM((KBLK * COLB,), jnp.int32),
            pltpu.SMEM((devices_all,), jnp.int32),
        ],
        compiler_params=pltpu.CompilerParams(vmem_limit_bytes=60 * 1024 * 1024),
        cost_estimate=pl.CostEstimate(flops=flops, bytes_accessed=tile_bytes + partial_bytes, transcendentals=0),
    )(left_flat, right_flat, owners[0], left_here, right_here)
    outgoing = pl.pallas_call(
        second_kernel,
        out_shape=jax.ShapeDtypeStruct((slots, side, side), jnp.bfloat16),
        in_specs=[smem, smem, smem, smem, vmem, vmem, anywhere],
        out_specs=anywhere,
        scratch_shapes=work + [
            pltpu.VMEM((2, ROWB * side, COL_GROUP * side), jnp.float32),
            pltpu.VMEM((products, side, side), jnp.bfloat16),
            pltpu.VMEM((side, side), jnp.bfloat16),
            pltpu.SemaphoreType.DMA((2,)),
            pltpu.SemaphoreType.DMA((slots,)),
        ],
        compiler_params=pltpu.CompilerParams(vmem_limit_bytes=60 * 1024 * 1024),
        cost_estimate=pl.CostEstimate(
            flops=flops, bytes_accessed=tile_bytes + partial_bytes + slots * side * side * 2, transcendentals=0
        ),
    )(slot_of, filled, left_index, right_index, left_next, right_next, partial)
    outgoing = outgoing.reshape(devices_all, capacity, side, side)
    received = lax.all_to_all(outgoing, ("row", "col"), split_axis=0, concat_axis=0, tiled=True)
    return received[None]


def solution(mesh):
    placed = (
        P("row", "col", None, None, None),
        P(),
        P("row", "col", None, None, None),
        P(),
        P(("row", "col"), None),
    )
    return jax.shard_map(
        body,
        mesh=mesh,
        in_specs=placed,
        out_specs=P(("row", "col"), None, None, None, None),
        check_vma=False,
    )
```

```python
import functools

import jax
import jax.numpy as jnp
from jax import lax
from jax.experimental import pallas as pl
from jax.experimental.pallas import tpu as pltpu
from jax.sharding import PartitionSpec as P

ROWB = 8
KBLK = 16
COLB = 16
COL_GROUP = 2
ROW_GROUP = 8


def from_behind(block, axis, distance):
    devices = range(lax.axis_size(axis))
    route = [((i - distance) % len(devices), i) for i in devices]
    return lax.ppermute(block, axis, route)


def fill(ref, count, value):
    def step(i, carry):
        ref[i] = value
        return carry

    lax.fori_loop(0, count, step, 0)


def invert_places(places, tile, index_ref, positions, stored):
    fill(index_ref, positions, -1)

    def step(n, carry):
        index_ref[places[tile[0], tile[1], n]] = n
        return carry

    lax.fori_loop(0, stored, step, 0)


def multiply_tiles(left_tile, right_tile, left_index, right_index, left_dense, right_column, emit, before=None):
    side = left_tile.shape[-1]
    zero_block = jnp.zeros((side, side), left_tile.dtype)

    def densify_left(r, carry):
        rows = pl.ds(pl.multiple_of(r * side, side), side)
        for k in range(KBLK):
            index = left_index[r * KBLK + k]
            block = left_tile[jnp.maximum(index, 0)]
            left_dense[rows, k * side:(k + 1) * side] = jnp.where(index >= 0, block, zero_block)
        return carry

    lax.fori_loop(0, ROWB, densify_left, 0)

    def column_pair(cp, carry):
        if before is not None:
            before(cp)
        for k in range(KBLK):
            for cc in range(COL_GROUP):
                index = right_index[k * COLB + cp * COL_GROUP + cc]
                block = right_tile[jnp.maximum(index, 0)]
                right_column[k * side:(k + 1) * side, cc * side:(cc + 1) * side] = jnp.where(
                    index >= 0, block, zero_block
                )

        def row_pair(rp, inner):
            rows = pl.ds(pl.multiple_of(rp * ROW_GROUP * side, ROW_GROUP * side), ROW_GROUP * side)
            result = jnp.dot(left_dense[rows, :], right_column[...], preferred_element_type=jnp.float32)
            emit(rp, cp, rows, result)
            return inner

        lax.fori_loop(0, ROWB // ROW_GROUP, row_pair, 0)
        return carry

    lax.fori_loop(0, COLB // COL_GROUP, column_pair, 0)


def first_kernel(
    rows_grid, cols_grid, capacity,
    left_places, right_places, owners, left_tile, right_tile,
    partial, slot_of, filled, left_index_next, right_index_next,
    left_dense, right_column, left_index, right_index, counts,
):
    side = left_tile.shape[-1]
    stored = left_tile.shape[0]
    row_here = lax.axis_index("row")
    col_here = lax.axis_index("col")
    row_next = lax.rem(row_here + 1, rows_grid)
    col_next = lax.rem(col_here + 1, cols_grid)
    invert_places(left_places, (row_here, col_here), left_index, ROWB * KBLK, stored)
    invert_places(right_places, (row_here, col_here), right_index, KBLK * COLB, stored)
    invert_places(left_places, (row_here, col_next), left_index_next, ROWB * KBLK, stored)
    invert_places(right_places, (row_next, col_here), right_index_next, KBLK * COLB, stored)
    fill(filled, filled.shape[0], 0)
    fill(counts, counts.shape[0], 0)

    def assign(m, carry):
        owner = owners[m]
        taken = counts[owner]
        slot = owner * capacity + taken
        slot_of[m] = slot
        filled[slot] = 1
        counts[owner] = taken + 1
        return carry

    lax.fori_loop(0, ROWB * COLB, assign, 0)

    def emit(rp, cp, rows, result):
        partial[cp, rows, :] = result

    multiply_tiles(left_tile, right_tile, left_index, right_index, left_dense, right_column, emit)


def second_kernel(
    slot_of, filled, left_index, right_index, left_tile, right_tile, partial,
    out,
    left_dense, right_column, partial_buf, staging, zero_ref, partial_sems, out_sems,
):
    side = left_tile.shape[-1]
    pairs = COLB // COL_GROUP
    slots = out.shape[0]
    zero_ref[...] = jnp.zeros(zero_ref.shape, zero_ref.dtype)

    def partial_copy(cp, buffer):
        return pltpu.make_async_copy(partial.at[cp], partial_buf.at[buffer], partial_sems.at[buffer])

    partial_copy(0, 0).start()

    def zero_slot(s, carry):
        @pl.when(filled[s] == 0)
        def _():
            pltpu.make_async_copy(zero_ref, out.at[s], out_sems.at[s]).start()

        return carry

    lax.fori_loop(0, slots, zero_slot, 0)

    def send_pair(cp):
        for r in range(ROWB):
            for cc in range(COL_GROUP):
                m = r * COLB + cp * COL_GROUP + cc
                slot = slot_of[m]
                pltpu.make_async_copy(staging.at[m], out.at[slot], out_sems.at[slot]).start()

    def before(cp):
        buffer = lax.rem(cp, 2)

        @pl.when(cp + 1 < pairs)
        def _():
            partial_copy(cp + 1, 1 - buffer).start()

        @pl.when(cp > 0)
        def _():
            send_pair(cp - 1)

        partial_copy(cp, buffer).wait()

    def emit(rp, cp, rows, result):
        buffer = lax.rem(cp, 2)
        total = result + partial_buf[buffer, rows, :]
        for rr in range(ROW_GROUP):
            for cc in range(COL_GROUP):
                m = (rp * ROW_GROUP + rr) * COLB + cp * COL_GROUP + cc
                piece = total[rr * side:(rr + 1) * side, cc * side:(cc + 1) * side]
                staging[m] = piece.astype(staging.dtype)

    multiply_tiles(left_tile, right_tile, left_index, right_index, left_dense, right_column, emit, before)
    send_pair(pairs - 1)

    def wait_slot(s, carry):
        pltpu.make_async_copy(zero_ref, out.at[s], out_sems.at[s]).wait()
        return carry

    lax.fori_loop(0, slots, wait_slot, 0)


def body(left_values, left_places, right_values, right_places, owners):
    rows_grid = lax.axis_size("row")
    cols_grid = lax.axis_size("col")
    devices_all = rows_grid * cols_grid
    left_here = left_values[0, 0]
    right_here = right_values[0, 0]
    side = left_here.shape[-1]
    left_next = from_behind(left_here, "col", -1)
    right_next = from_behind(right_here, "row", -1)
    capacity = 2 * ROWB * COLB // devices_all
    slots = devices_all * capacity
    products = ROWB * COLB
    pairs = COLB // COL_GROUP
    smem = pl.BlockSpec(memory_space=pltpu.SMEM)
    vmem = pl.BlockSpec(memory_space=pltpu.VMEM)
    anywhere = pl.BlockSpec(memory_space=pl.ANY)
    work = [
        pltpu.VMEM((ROWB * side, KBLK * side), jnp.bfloat16),
        pltpu.VMEM((KBLK * side, COL_GROUP * side), jnp.bfloat16),
    ]
    flops = 2 * (ROWB * side) * (KBLK * side) * (COLB * side)
    tile_bytes = 2 * left_here.size * 2
    partial_bytes = ROWB * COLB * side * side * 4
    partial, slot_of, filled, left_index, right_index = pl.pallas_call(
        functools.partial(first_kernel, rows_grid, cols_grid, capacity),
        out_shape=(
            jax.ShapeDtypeStruct((pairs, ROWB * side, COL_GROUP * side), jnp.float32),
            jax.ShapeDtypeStruct((products,), jnp.int32),
            jax.ShapeDtypeStruct((slots,), jnp.int32),
            jax.ShapeDtypeStruct((ROWB * KBLK,), jnp.int32),
            jax.ShapeDtypeStruct((KBLK * COLB,), jnp.int32),
        ),
        in_specs=[smem, smem, smem, vmem, vmem],
        out_specs=(vmem, smem, smem, smem, smem),
        scratch_shapes=work + [
            pltpu.SMEM((ROWB * KBLK,), jnp.int32),
            pltpu.SMEM((KBLK * COLB,), jnp.int32),
            pltpu.SMEM((devices_all,), jnp.int32),
        ],
        compiler_params=pltpu.CompilerParams(vmem_limit_bytes=60 * 1024 * 1024),
        cost_estimate=pl.CostEstimate(flops=flops, bytes_accessed=tile_bytes + partial_bytes, transcendentals=0),
    )(left_places, right_places, owners[0], left_here, right_here)
    outgoing = pl.pallas_call(
        second_kernel,
        out_shape=jax.ShapeDtypeStruct((slots, side, side), jnp.bfloat16),
        in_specs=[smem, smem, smem, smem, vmem, vmem, anywhere],
        out_specs=anywhere,
        scratch_shapes=work + [
            pltpu.VMEM((2, ROWB * side, COL_GROUP * side), jnp.float32),
            pltpu.VMEM((products, side, side), jnp.bfloat16),
            pltpu.VMEM((side, side), jnp.bfloat16),
            pltpu.SemaphoreType.DMA((2,)),
            pltpu.SemaphoreType.DMA((slots,)),
        ],
        compiler_params=pltpu.CompilerParams(vmem_limit_bytes=60 * 1024 * 1024),
        cost_estimate=pl.CostEstimate(
            flops=flops, bytes_accessed=tile_bytes + partial_bytes + slots * side * side * 2, transcendentals=0
        ),
    )(slot_of, filled, left_index, right_index, left_next, right_next, partial)
    outgoing = outgoing.reshape(devices_all, capacity, side, side)
    received = lax.all_to_all(outgoing, ("row", "col"), split_axis=0, concat_axis=0, tiled=True)
    return received[None]


def solution(mesh):
    placed = (
        P("row", "col", None, None, None),
        P(),
        P("row", "col", None, None, None),
        P(),
        P(("row", "col"), None),
    )
    return jax.shard_map(
        body,
        mesh=mesh,
        in_specs=placed,
        out_specs=P(("row", "col"), None, None, None, None),
        check_vma=False,
    )
```

```python
import functools

import jax
import jax.numpy as jnp
from jax import lax
from jax.experimental import pallas as pl
from jax.experimental.pallas import tpu as pltpu
from jax.sharding import PartitionSpec as P

ROWB = 8
KBLK = 16
COLB = 16
COL_GROUP = 2
ROW_GROUP = 8


def from_behind(block, axis, distance):
    devices = range(lax.axis_size(axis))
    route = [((i - distance) % len(devices), i) for i in devices]
    return lax.ppermute(block, axis, route)


def fill(ref, count, value):
    def step(i, carry):
        ref[i] = value
        return carry

    lax.fori_loop(0, count, step, 0)


def invert_places(places, tile, index_ref, positions, stored):
    fill(index_ref, positions, -1)

    def step(n, carry):
        index_ref[places[tile[0], tile[1], n]] = n
        return carry

    lax.fori_loop(0, stored, step, 0)


def multiply_tiles(left_tile, right_tile, left_index, right_index, left_dense, right_column, emit, before=None):
    side = left_tile.shape[-1]
    zero_block = jnp.zeros((side, side), left_tile.dtype)

    def densify_left(r, carry):
        rows = pl.ds(pl.multiple_of(r * side, side), side)
        for k in range(KBLK):
            index = left_index[r * KBLK + k]
            block = left_tile[jnp.maximum(index, 0)]
            left_dense[rows, k * side:(k + 1) * side] = jnp.where(index >= 0, block, zero_block)
        return carry

    lax.fori_loop(0, ROWB, densify_left, 0)

    right_column[...] = jnp.zeros(right_column.shape, right_column.dtype)

    def place_column(cp, clear):
        for k in range(KBLK):
            for cc in range(COL_GROUP):
                index = right_index[k * COLB + cp * COL_GROUP + cc]

                @pl.when(index >= 0)
                def _():
                    block = zero_block if clear else right_tile[index]
                    right_column[k * side:(k + 1) * side, cc * side:(cc + 1) * side] = block

    def column_pair(cp, carry):
        if before is not None:
            before(cp)
        place_column(cp, False)

        def row_pair(rp, inner):
            rows = pl.ds(pl.multiple_of(rp * ROW_GROUP * side, ROW_GROUP * side), ROW_GROUP * side)
            result = jnp.dot(left_dense[rows, :], right_column[...], preferred_element_type=jnp.float32)
            emit(rp, cp, rows, result)
            return inner

        lax.fori_loop(0, ROWB // ROW_GROUP, row_pair, 0)
        place_column(cp, True)
        return carry

    lax.fori_loop(0, COLB // COL_GROUP, column_pair, 0)


def first_kernel(
    rows_grid, cols_grid, capacity,
    left_places, right_places, owners, left_tile, right_tile,
    partial, slot_of, left_index_next, right_index_next, outgoing,
    left_dense, right_column, left_index, right_index, counts, filled, zero_ref, zero_sems,
):
    side = left_tile.shape[-1]
    stored = left_tile.shape[0]
    row_here = lax.axis_index("row")
    col_here = lax.axis_index("col")
    row_next = lax.rem(row_here + 1, rows_grid)
    col_next = lax.rem(col_here + 1, cols_grid)
    invert_places(left_places, (row_here, col_here), left_index, ROWB * KBLK, stored)
    invert_places(right_places, (row_here, col_here), right_index, KBLK * COLB, stored)
    invert_places(left_places, (row_here, col_next), left_index_next, ROWB * KBLK, stored)
    invert_places(right_places, (row_next, col_here), right_index_next, KBLK * COLB, stored)
    fill(filled, filled.shape[0], 0)
    fill(counts, counts.shape[0], 0)

    def assign(m, carry):
        owner = owners[m]
        taken = counts[owner]
        slot = owner * capacity + taken
        slot_of[m] = slot
        filled[slot] = 1
        counts[owner] = taken + 1
        return carry

    lax.fori_loop(0, ROWB * COLB, assign, 0)
    zero_ref[...] = jnp.zeros(zero_ref.shape, zero_ref.dtype)

    def zero_slot(s, carry):
        @pl.when(filled[s] == 0)
        def _():
            pltpu.make_async_copy(zero_ref, outgoing.at[s], zero_sems.at[s]).start()

        return carry

    lax.fori_loop(0, outgoing.shape[0], zero_slot, 0)

    def emit(rp, cp, rows, result):
        partial[cp, rows, :] = result

    multiply_tiles(left_tile, right_tile, left_index, right_index, left_dense, right_column, emit)

    def wait_slot(s, carry):
        @pl.when(filled[s] == 0)
        def _():
            pltpu.make_async_copy(zero_ref, outgoing.at[s], zero_sems.at[s]).wait()

        return carry

    lax.fori_loop(0, outgoing.shape[0], wait_slot, 0)


def second_kernel(
    slot_of, left_index, right_index, left_tile, right_tile, partial, outgoing,
    out,
    left_dense, right_column, partial_buf, staging, partial_sems, out_sems,
):
    side = left_tile.shape[-1]
    pairs = COLB // COL_GROUP
    products = ROWB * COLB

    def partial_copy(cp, buffer):
        return pltpu.make_async_copy(partial.at[cp], partial_buf.at[buffer], partial_sems.at[buffer])

    partial_copy(0, 0).start()

    def send_pair(cp):
        for r in range(ROWB):
            for cc in range(COL_GROUP):
                m = r * COLB + cp * COL_GROUP + cc
                pltpu.make_async_copy(staging.at[m], out.at[slot_of[m]], out_sems.at[m]).start()

    def before(cp):
        buffer = lax.rem(cp, 2)

        @pl.when(cp + 1 < pairs)
        def _():
            partial_copy(cp + 1, 1 - buffer).start()

        @pl.when(cp > 0)
        def _():
            send_pair(cp - 1)

        partial_copy(cp, buffer).wait()

    def emit(rp, cp, rows, result):
        buffer = lax.rem(cp, 2)
        total = result + partial_buf[buffer, rows, :]
        for rr in range(ROW_GROUP):
            for cc in range(COL_GROUP):
                m = (rp * ROW_GROUP + rr) * COLB + cp * COL_GROUP + cc
                piece = total[rr * side:(rr + 1) * side, cc * side:(cc + 1) * side]
                staging[m] = piece.astype(staging.dtype)

    multiply_tiles(left_tile, right_tile, left_index, right_index, left_dense, right_column, emit, before)
    send_pair(pairs - 1)

    def wait_block(m, carry):
        pltpu.make_async_copy(staging.at[m], out.at[slot_of[m]], out_sems.at[m]).wait()
        return carry

    lax.fori_loop(0, products, wait_block, 0)


def body(left_values, left_places, right_values, right_places, owners):
    rows_grid = lax.axis_size("row")
    cols_grid = lax.axis_size("col")
    devices_all = rows_grid * cols_grid
    left_here = left_values[0, 0]
    right_here = right_values[0, 0]
    side = left_here.shape[-1]
    left_next = from_behind(left_here, "col", -1)
    right_next = from_behind(right_here, "row", -1)
    capacity = 2 * ROWB * COLB // devices_all
    slots = devices_all * capacity
    products = ROWB * COLB
    pairs = COLB // COL_GROUP
    smem = pl.BlockSpec(memory_space=pltpu.SMEM)
    vmem = pl.BlockSpec(memory_space=pltpu.VMEM)
    anywhere = pl.BlockSpec(memory_space=pl.ANY)
    work = [
        pltpu.VMEM((ROWB * side, KBLK * side), jnp.bfloat16),
        pltpu.VMEM((KBLK * side, COL_GROUP * side), jnp.bfloat16),
    ]
    flops = 2 * (ROWB * side) * (KBLK * side) * (COLB * side)
    tile_bytes = 2 * left_here.size * 2
    partial_bytes = ROWB * COLB * side * side * 4
    partial, slot_of, left_index, right_index, outgoing = pl.pallas_call(
        functools.partial(first_kernel, rows_grid, cols_grid, capacity),
        out_shape=(
            jax.ShapeDtypeStruct((pairs, ROWB * side, COL_GROUP * side), jnp.float32),
            jax.ShapeDtypeStruct((products,), jnp.int32),
            jax.ShapeDtypeStruct((ROWB * KBLK,), jnp.int32),
            jax.ShapeDtypeStruct((KBLK * COLB,), jnp.int32),
            jax.ShapeDtypeStruct((slots, side, side), jnp.bfloat16),
        ),
        in_specs=[smem, smem, smem, vmem, vmem],
        out_specs=(vmem, smem, smem, smem, anywhere),
        scratch_shapes=work + [
            pltpu.SMEM((ROWB * KBLK,), jnp.int32),
            pltpu.SMEM((KBLK * COLB,), jnp.int32),
            pltpu.SMEM((devices_all,), jnp.int32),
            pltpu.SMEM((slots,), jnp.int32),
            pltpu.VMEM((side, side), jnp.bfloat16),
            pltpu.SemaphoreType.DMA((slots,)),
        ],
        compiler_params=pltpu.CompilerParams(vmem_limit_bytes=60 * 1024 * 1024),
        cost_estimate=pl.CostEstimate(flops=flops, bytes_accessed=tile_bytes + partial_bytes, transcendentals=0),
    )(left_places, right_places, owners[0], left_here, right_here)
    outgoing = pl.pallas_call(
        second_kernel,
        out_shape=jax.ShapeDtypeStruct((slots, side, side), jnp.bfloat16),
        in_specs=[smem, smem, smem, vmem, vmem, anywhere, anywhere],
        out_specs=anywhere,
        input_output_aliases={6: 0},
        scratch_shapes=work + [
            pltpu.VMEM((2, ROWB * side, COL_GROUP * side), jnp.float32),
            pltpu.VMEM((products, side, side), jnp.bfloat16),
            pltpu.SemaphoreType.DMA((2,)),
            pltpu.SemaphoreType.DMA((products,)),
        ],
        compiler_params=pltpu.CompilerParams(vmem_limit_bytes=60 * 1024 * 1024),
        cost_estimate=pl.CostEstimate(
            flops=flops, bytes_accessed=tile_bytes + partial_bytes + slots * side * side * 2, transcendentals=0
        ),
    )(slot_of, left_index, right_index, left_next, right_next, partial, outgoing)
    outgoing = outgoing.reshape(devices_all, capacity, side, side)
    received = lax.all_to_all(outgoing, ("row", "col"), split_axis=0, concat_axis=0, tiled=True)
    return received[None]


def solution(mesh):
    placed = (
        P("row", "col", None, None, None),
        P(),
        P("row", "col", None, None, None),
        P(),
        P(("row", "col"), None),
    )
    return jax.shard_map(
        body,
        mesh=mesh,
        in_specs=placed,
        out_specs=P(("row", "col"), None, None, None, None),
        check_vma=False,
    )
```

```python
import functools

import jax
import jax.numpy as jnp
from jax import lax
from jax.experimental import pallas as pl
from jax.experimental.pallas import tpu as pltpu
from jax.sharding import PartitionSpec as P

ROWB = 8
KBLK = 16
COLB = 16
COL_GROUP = 2
ROW_GROUP = 8
COPY_STEPS = 8


def from_behind(block, axis, distance):
    devices = range(lax.axis_size(axis))
    route = [((i - distance) % len(devices), i) for i in devices]
    return lax.ppermute(block, axis, route)


def fill(ref, count, value):
    def step(i, carry):
        ref[i] = value
        return carry

    lax.fori_loop(0, count, step, 0)


def invert_places(places, tile, index_ref, positions, stored):
    fill(index_ref, positions, -1)

    def step(n, carry):
        index_ref[places[tile[0], tile[1], n]] = n
        return carry

    lax.fori_loop(0, stored, step, 0)


def multiply_tiles(left_tile, right_tile, left_index, right_index, left_dense, right_column, emit, before=None):
    side = left_tile.shape[-1]
    zero_block = jnp.zeros((side, side), left_tile.dtype)

    def densify_left(r, carry):
        rows = pl.ds(pl.multiple_of(r * side, side), side)
        for k in range(KBLK):
            index = left_index[r * KBLK + k]
            block = left_tile[jnp.maximum(index, 0)]
            left_dense[rows, k * side:(k + 1) * side] = jnp.where(index >= 0, block, zero_block)
        return carry

    lax.fori_loop(0, ROWB, densify_left, 0)

    right_column[...] = jnp.zeros(right_column.shape, right_column.dtype)

    def place_column(cp, clear):
        for k in range(KBLK):
            for cc in range(COL_GROUP):
                index = right_index[k * COLB + cp * COL_GROUP + cc]

                @pl.when(index >= 0)
                def _():
                    block = zero_block if clear else right_tile[index]
                    right_column[k * side:(k + 1) * side, cc * side:(cc + 1) * side] = block

    def column_pair(cp, carry):
        if before is not None:
            before(cp)
        place_column(cp, False)

        def row_pair(rp, inner):
            rows = pl.ds(pl.multiple_of(rp * ROW_GROUP * side, ROW_GROUP * side), ROW_GROUP * side)
            result = jnp.dot(left_dense[rows, :], right_column[...], preferred_element_type=jnp.float32)
            emit(rp, cp, rows, result)
            return inner

        lax.fori_loop(0, ROWB // ROW_GROUP, row_pair, 0)
        place_column(cp, True)
        return carry

    lax.fori_loop(0, COLB // COL_GROUP, column_pair, 0)


def first_kernel(
    rows_grid, cols_grid, capacity,
    left_places, right_places, owners, left_tile, right_tile,
    partial, slot_of, left_index_next, right_index_next, outgoing,
    left_dense, right_column, left_index, right_index, counts, filled, zero_ref, zero_sems,
):
    side = left_tile.shape[-1]
    stored = left_tile.shape[0]
    row_here = lax.axis_index("row")
    col_here = lax.axis_index("col")
    row_next = lax.rem(row_here + 1, rows_grid)
    col_next = lax.rem(col_here + 1, cols_grid)
    invert_places(left_places, (row_here, col_here), left_index, ROWB * KBLK, stored)
    invert_places(right_places, (row_here, col_here), right_index, KBLK * COLB, stored)
    invert_places(left_places, (row_here, col_next), left_index_next, ROWB * KBLK, stored)
    invert_places(right_places, (row_next, col_here), right_index_next, KBLK * COLB, stored)
    fill(filled, filled.shape[0], 0)
    fill(counts, counts.shape[0], 0)

    def assign(m, carry):
        owner = owners[m]
        taken = counts[owner]
        slot = owner * capacity + taken
        slot_of[m] = slot
        filled[slot] = 1
        counts[owner] = taken + 1
        return carry

    lax.fori_loop(0, ROWB * COLB, assign, 0)
    zero_ref[...] = jnp.zeros(zero_ref.shape, zero_ref.dtype)

    def zero_slot(s, carry):
        @pl.when(filled[s] == 0)
        def _():
            pltpu.make_async_copy(zero_ref, outgoing.at[s], zero_sems.at[s]).start()

        return carry

    lax.fori_loop(0, outgoing.shape[0], zero_slot, 0)

    def emit(rp, cp, rows, result):
        partial[cp, rows, :] = result

    multiply_tiles(left_tile, right_tile, left_index, right_index, left_dense, right_column, emit)

    def wait_slot(s, carry):
        @pl.when(filled[s] == 0)
        def _():
            pltpu.make_async_copy(zero_ref, outgoing.at[s], zero_sems.at[s]).wait()

        return carry

    lax.fori_loop(0, outgoing.shape[0], wait_slot, 0)


def second_kernel(
    slot_of, left_index, right_index, left_tile, right_tile, partial, outgoing,
    out,
    left_dense, right_column, partial_buf, staging, partial_sems, out_sems,
):
    side = left_tile.shape[-1]
    pairs = COLB // COL_GROUP
    products = ROWB * COLB

    def partial_copy(cp, buffer):
        return pltpu.make_async_copy(partial.at[cp], partial_buf.at[buffer], partial_sems.at[buffer])

    partial_copy(0, 0).start()

    def send_pair(cp):
        for r in range(ROWB):
            for cc in range(COL_GROUP):
                m = r * COLB + cp * COL_GROUP + cc
                pltpu.make_async_copy(staging.at[m], out.at[slot_of[m]], out_sems.at[m]).start()

    def before(cp):
        buffer = lax.rem(cp, 2)

        @pl.when(cp + 1 < pairs)
        def _():
            partial_copy(cp + 1, 1 - buffer).start()

        @pl.when(cp > 0)
        def _():
            send_pair(cp - 1)

        partial_copy(cp, buffer).wait()

    def emit(rp, cp, rows, result):
        buffer = lax.rem(cp, 2)
        total = result + partial_buf[buffer, rows, :]
        for rr in range(ROW_GROUP):
            for cc in range(COL_GROUP):
                m = (rp * ROW_GROUP + rr) * COLB + cp * COL_GROUP + cc
                piece = total[rr * side:(rr + 1) * side, cc * side:(cc + 1) * side]
                staging[m] = piece.astype(staging.dtype)

    multiply_tiles(left_tile, right_tile, left_index, right_index, left_dense, right_column, emit, before)
    send_pair(pairs - 1)

    def wait_block(m, carry):
        pltpu.make_async_copy(staging.at[m], out.at[slot_of[m]], out_sems.at[m]).wait()
        return carry

    lax.fori_loop(0, products, wait_block, 0)


def pass_through(source, target):
    target[...] = source[...]


def body(left_values, left_places, right_values, right_places, owners):
    rows_grid = lax.axis_size("row")
    cols_grid = lax.axis_size("col")
    devices_all = rows_grid * cols_grid
    left_here = left_values[0, 0]
    right_here = right_values[0, 0]
    side = left_here.shape[-1]
    left_next = from_behind(left_here, "col", -1)
    right_next = from_behind(right_here, "row", -1)
    capacity = 2 * ROWB * COLB // devices_all
    slots = devices_all * capacity
    products = ROWB * COLB
    pairs = COLB // COL_GROUP
    smem = pl.BlockSpec(memory_space=pltpu.SMEM)
    vmem = pl.BlockSpec(memory_space=pltpu.VMEM)
    anywhere = pl.BlockSpec(memory_space=pl.ANY)
    work = [
        pltpu.VMEM((ROWB * side, KBLK * side), jnp.bfloat16),
        pltpu.VMEM((KBLK * side, COL_GROUP * side), jnp.bfloat16),
    ]
    flops = 2 * (ROWB * side) * (KBLK * side) * (COLB * side)
    tile_bytes = 2 * left_here.size * 2
    partial_bytes = ROWB * COLB * side * side * 4
    partial, slot_of, left_index, right_index, outgoing = pl.pallas_call(
        functools.partial(first_kernel, rows_grid, cols_grid, capacity),
        out_shape=(
            jax.ShapeDtypeStruct((pairs, ROWB * side, COL_GROUP * side), jnp.float32),
            jax.ShapeDtypeStruct((products,), jnp.int32),
            jax.ShapeDtypeStruct((ROWB * KBLK,), jnp.int32),
            jax.ShapeDtypeStruct((KBLK * COLB,), jnp.int32),
            jax.ShapeDtypeStruct((slots, side, side), jnp.bfloat16),
        ),
        in_specs=[smem, smem, smem, vmem, vmem],
        out_specs=(vmem, smem, smem, smem, anywhere),
        scratch_shapes=work + [
            pltpu.SMEM((ROWB * KBLK,), jnp.int32),
            pltpu.SMEM((KBLK * COLB,), jnp.int32),
            pltpu.SMEM((devices_all,), jnp.int32),
            pltpu.SMEM((slots,), jnp.int32),
            pltpu.VMEM((side, side), jnp.bfloat16),
            pltpu.SemaphoreType.DMA((slots,)),
        ],
        compiler_params=pltpu.CompilerParams(vmem_limit_bytes=60 * 1024 * 1024),
        cost_estimate=pl.CostEstimate(flops=flops, bytes_accessed=tile_bytes + partial_bytes, transcendentals=0),
    )(left_places, right_places, owners[0], left_here, right_here)
    outgoing = pl.pallas_call(
        second_kernel,
        out_shape=jax.ShapeDtypeStruct((slots, side, side), jnp.bfloat16),
        in_specs=[smem, smem, smem, vmem, vmem, anywhere, anywhere],
        out_specs=anywhere,
        input_output_aliases={6: 0},
        scratch_shapes=work + [
            pltpu.VMEM((2, ROWB * side, COL_GROUP * side), jnp.float32),
            pltpu.VMEM((products, side, side), jnp.bfloat16),
            pltpu.SemaphoreType.DMA((2,)),
            pltpu.SemaphoreType.DMA((products,)),
        ],
        compiler_params=pltpu.CompilerParams(vmem_limit_bytes=60 * 1024 * 1024),
        cost_estimate=pl.CostEstimate(
            flops=flops, bytes_accessed=tile_bytes + partial_bytes + slots * side * side * 2, transcendentals=0
        ),
    )(slot_of, left_index, right_index, left_next, right_next, partial, outgoing)
    outgoing = outgoing.reshape(devices_all, capacity, side, side)
    received = lax.all_to_all(outgoing, ("row", "col"), split_axis=0, concat_axis=0, tiled=True)
    chunk = devices_all // COPY_STEPS
    block = pl.BlockSpec((chunk, capacity, side, side), lambda i: (i, 0, 0, 0))
    received = pl.pallas_call(
        pass_through,
        out_shape=jax.ShapeDtypeStruct(received.shape, received.dtype),
        grid=(COPY_STEPS,),
        in_specs=[block],
        out_specs=block,
        cost_estimate=pl.CostEstimate(flops=0, bytes_accessed=2 * received.size * 2, transcendentals=0),
    )(received)
    return received[None]


def solution(mesh):
    placed = (
        P("row", "col", None, None, None),
        P(),
        P("row", "col", None, None, None),
        P(),
        P(("row", "col"), None),
    )
    return jax.shard_map(
        body,
        mesh=mesh,
        in_specs=placed,
        out_specs=P(("row", "col"), None, None, None, None),
        check_vma=False,
    )
```

```python
import functools

import jax
import jax.numpy as jnp
from jax import lax
from jax.experimental import pallas as pl
from jax.experimental.pallas import tpu as pltpu
from jax.sharding import PartitionSpec as P

ROWB = 8
KBLK = 16
COLB = 16
COL_GROUP = 2
ROW_GROUP = 8
COPY_STEPS = 32


def from_behind(block, axis, distance):
    devices = range(lax.axis_size(axis))
    route = [((i - distance) % len(devices), i) for i in devices]
    return lax.ppermute(block, axis, route)


def fill(ref, count, value):
    def step(i, carry):
        ref[i] = value
        return carry

    lax.fori_loop(0, count, step, 0)


def invert_places(places, tile, index_ref, positions, stored):
    fill(index_ref, positions, -1)

    def step(n, carry):
        index_ref[places[tile[0], tile[1], n]] = n
        return carry

    lax.fori_loop(0, stored, step, 0)


def multiply_tiles(
    left_tile, right_tile, left_index, right_index, left_dense, right_column, emit, before=None,
    left_ready=None, right_ready=None,
):
    side = left_tile.shape[-1]
    zero_block = jnp.zeros((side, side), left_tile.dtype)
    right_column[...] = jnp.zeros(right_column.shape, right_column.dtype)
    if left_ready is not None:
        left_ready()

    def densify_left(r, carry):
        rows = pl.ds(pl.multiple_of(r * side, side), side)
        for k in range(KBLK):
            index = left_index[r * KBLK + k]
            block = left_tile[jnp.maximum(index, 0)]
            left_dense[rows, k * side:(k + 1) * side] = jnp.where(index >= 0, block, zero_block)
        return carry

    lax.fori_loop(0, ROWB, densify_left, 0)
    if right_ready is not None:
        right_ready()

    def place_column(cp, clear):
        for k in range(KBLK):
            for cc in range(COL_GROUP):
                index = right_index[k * COLB + cp * COL_GROUP + cc]

                @pl.when(index >= 0)
                def _():
                    block = zero_block if clear else right_tile[index]
                    right_column[k * side:(k + 1) * side, cc * side:(cc + 1) * side] = block

    def column_pair(cp, carry):
        if before is not None:
            before(cp)
        place_column(cp, False)

        def row_pair(rp, inner):
            rows = pl.ds(pl.multiple_of(rp * ROW_GROUP * side, ROW_GROUP * side), ROW_GROUP * side)
            result = jnp.dot(left_dense[rows, :], right_column[...], preferred_element_type=jnp.float32)
            emit(rp, cp, rows, result)
            return inner

        lax.fori_loop(0, ROWB // ROW_GROUP, row_pair, 0)
        place_column(cp, True)
        return carry

    lax.fori_loop(0, COLB // COL_GROUP, column_pair, 0)


def first_kernel(
    rows_grid, cols_grid, capacity,
    left_places, right_places, owners, left_tile, right_tile,
    partial, slot_of, left_index_next, right_index_next, outgoing,
    left_dense, right_column, left_index, right_index, counts, filled, zero_ref, zero_sems,
):
    side = left_tile.shape[-1]
    stored = left_tile.shape[0]
    row_here = lax.axis_index("row")
    col_here = lax.axis_index("col")
    row_next = lax.rem(row_here + 1, rows_grid)
    col_next = lax.rem(col_here + 1, cols_grid)
    invert_places(left_places, (row_here, col_here), left_index, ROWB * KBLK, stored)
    invert_places(right_places, (row_here, col_here), right_index, KBLK * COLB, stored)
    invert_places(left_places, (row_here, col_next), left_index_next, ROWB * KBLK, stored)
    invert_places(right_places, (row_next, col_here), right_index_next, KBLK * COLB, stored)
    fill(filled, filled.shape[0], 0)
    fill(counts, counts.shape[0], 0)

    def assign(m, carry):
        owner = owners[m]
        taken = counts[owner]
        slot = owner * capacity + taken
        slot_of[m] = slot
        filled[slot] = 1
        counts[owner] = taken + 1
        return carry

    lax.fori_loop(0, ROWB * COLB, assign, 0)
    zero_ref[...] = jnp.zeros(zero_ref.shape, zero_ref.dtype)

    def zero_slot(s, carry):
        @pl.when(filled[s] == 0)
        def _():
            pltpu.make_async_copy(zero_ref, outgoing.at[s], zero_sems.at[s]).start()

        return carry

    lax.fori_loop(0, outgoing.shape[0], zero_slot, 0)

    def emit(rp, cp, rows, result):
        partial[cp, rows, :] = result

    multiply_tiles(left_tile, right_tile, left_index, right_index, left_dense, right_column, emit)

    def wait_slot(s, carry):
        @pl.when(filled[s] == 0)
        def _():
            pltpu.make_async_copy(zero_ref, outgoing.at[s], zero_sems.at[s]).wait()

        return carry

    lax.fori_loop(0, outgoing.shape[0], wait_slot, 0)


def second_kernel(
    slot_of, left_index, right_index, left_hbm, right_hbm, partial, outgoing,
    out,
    left_dense, right_column, partial_buf, staging, left_tile, right_tile, partial_sems, out_sems, tile_sems,
):
    side = left_tile.shape[-1]
    pairs = COLB // COL_GROUP
    products = ROWB * COLB
    left_copy = pltpu.make_async_copy(left_hbm, left_tile, tile_sems.at[0])
    right_copy = pltpu.make_async_copy(right_hbm, right_tile, tile_sems.at[1])
    left_copy.start()
    right_copy.start()

    def partial_copy(cp, buffer):
        return pltpu.make_async_copy(partial.at[cp], partial_buf.at[buffer], partial_sems.at[buffer])

    partial_copy(0, 0).start()

    def send_pair(cp):
        for r in range(ROWB):
            for cc in range(COL_GROUP):
                m = r * COLB + cp * COL_GROUP + cc
                pltpu.make_async_copy(staging.at[m], out.at[slot_of[m]], out_sems.at[m]).start()

    def before(cp):
        buffer = lax.rem(cp, 2)

        @pl.when(cp + 1 < pairs)
        def _():
            partial_copy(cp + 1, 1 - buffer).start()

        @pl.when(cp > 0)
        def _():
            send_pair(cp - 1)

        partial_copy(cp, buffer).wait()

    def emit(rp, cp, rows, result):
        buffer = lax.rem(cp, 2)
        total = result + partial_buf[buffer, rows, :]
        for rr in range(ROW_GROUP):
            for cc in range(COL_GROUP):
                m = (rp * ROW_GROUP + rr) * COLB + cp * COL_GROUP + cc
                piece = total[rr * side:(rr + 1) * side, cc * side:(cc + 1) * side]
                staging[m] = piece.astype(staging.dtype)

    multiply_tiles(
        left_tile, right_tile, left_index, right_index, left_dense, right_column, emit, before,
        left_copy.wait, right_copy.wait,
    )
    send_pair(pairs - 1)

    def wait_block(m, carry):
        pltpu.make_async_copy(staging.at[m], out.at[slot_of[m]], out_sems.at[m]).wait()
        return carry

    lax.fori_loop(0, products, wait_block, 0)


def pass_through(source, target):
    target[...] = source[...]


def body(left_values, left_places, right_values, right_places, owners):
    rows_grid = lax.axis_size("row")
    cols_grid = lax.axis_size("col")
    devices_all = rows_grid * cols_grid
    left_here = left_values[0, 0]
    right_here = right_values[0, 0]
    side = left_here.shape[-1]
    left_next = from_behind(left_here, "col", -1)
    right_next = from_behind(right_here, "row", -1)
    capacity = 2 * ROWB * COLB // devices_all
    slots = devices_all * capacity
    products = ROWB * COLB
    pairs = COLB // COL_GROUP
    smem = pl.BlockSpec(memory_space=pltpu.SMEM)
    vmem = pl.BlockSpec(memory_space=pltpu.VMEM)
    anywhere = pl.BlockSpec(memory_space=pl.ANY)
    work = [
        pltpu.VMEM((ROWB * side, KBLK * side), jnp.bfloat16),
        pltpu.VMEM((KBLK * side, COL_GROUP * side), jnp.bfloat16),
    ]
    flops = 2 * (ROWB * side) * (KBLK * side) * (COLB * side)
    tile_bytes = 2 * left_here.size * 2
    partial_bytes = ROWB * COLB * side * side * 4
    partial, slot_of, left_index, right_index, outgoing = pl.pallas_call(
        functools.partial(first_kernel, rows_grid, cols_grid, capacity),
        out_shape=(
            jax.ShapeDtypeStruct((pairs, ROWB * side, COL_GROUP * side), jnp.float32),
            jax.ShapeDtypeStruct((products,), jnp.int32),
            jax.ShapeDtypeStruct((ROWB * KBLK,), jnp.int32),
            jax.ShapeDtypeStruct((KBLK * COLB,), jnp.int32),
            jax.ShapeDtypeStruct((slots, side, side), jnp.bfloat16),
        ),
        in_specs=[smem, smem, smem, vmem, vmem],
        out_specs=(vmem, smem, smem, smem, anywhere),
        scratch_shapes=work + [
            pltpu.SMEM((ROWB * KBLK,), jnp.int32),
            pltpu.SMEM((KBLK * COLB,), jnp.int32),
            pltpu.SMEM((devices_all,), jnp.int32),
            pltpu.SMEM((slots,), jnp.int32),
            pltpu.VMEM((side, side), jnp.bfloat16),
            pltpu.SemaphoreType.DMA((slots,)),
        ],
        compiler_params=pltpu.CompilerParams(vmem_limit_bytes=60 * 1024 * 1024),
        cost_estimate=pl.CostEstimate(flops=flops, bytes_accessed=tile_bytes + partial_bytes, transcendentals=0),
    )(left_places, right_places, owners[0], left_here, right_here)
    outgoing = pl.pallas_call(
        second_kernel,
        out_shape=jax.ShapeDtypeStruct((slots, side, side), jnp.bfloat16),
        in_specs=[smem, smem, smem, anywhere, anywhere, anywhere, anywhere],
        out_specs=anywhere,
        input_output_aliases={6: 0},
        scratch_shapes=work + [
            pltpu.VMEM((2, ROWB * side, COL_GROUP * side), jnp.float32),
            pltpu.VMEM((products, side, side), jnp.bfloat16),
            pltpu.VMEM(left_here.shape, left_here.dtype),
            pltpu.VMEM(right_here.shape, right_here.dtype),
            pltpu.SemaphoreType.DMA((2,)),
            pltpu.SemaphoreType.DMA((products,)),
            pltpu.SemaphoreType.DMA((2,)),
        ],
        compiler_params=pltpu.CompilerParams(vmem_limit_bytes=60 * 1024 * 1024),
        cost_estimate=pl.CostEstimate(
            flops=flops, bytes_accessed=tile_bytes + partial_bytes + slots * side * side * 2, transcendentals=0
        ),
    )(slot_of, left_index, right_index, left_next, right_next, partial, outgoing)
    outgoing = outgoing.reshape(devices_all, capacity, side, side)
    received = lax.all_to_all(outgoing, ("row", "col"), split_axis=0, concat_axis=0, tiled=True)
    chunk = devices_all // COPY_STEPS
    block = pl.BlockSpec((chunk, capacity, side, side), lambda i: (i, 0, 0, 0))
    received = pl.pallas_call(
        pass_through,
        out_shape=jax.ShapeDtypeStruct(received.shape, received.dtype),
        grid=(COPY_STEPS,),
        in_specs=[block],
        out_specs=block,
        cost_estimate=pl.CostEstimate(flops=0, bytes_accessed=2 * received.size * 2, transcendentals=0),
    )(received)
    return received[None]


def solution(mesh):
    placed = (
        P("row", "col", None, None, None),
        P(),
        P("row", "col", None, None, None),
        P(),
        P(("row", "col"), None),
    )
    return jax.shard_map(
        body,
        mesh=mesh,
        in_specs=placed,
        out_specs=P(("row", "col"), None, None, None, None),
        check_vma=False,
    )
```

```python
import functools

import jax
import jax.numpy as jnp
from jax import lax
from jax.experimental import pallas as pl
from jax.experimental.pallas import tpu as pltpu
from jax.sharding import PartitionSpec as P

ROWB = 8
KBLK = 16
COLB = 16
COL_GROUP = 2
ROW_GROUP = 8
COPY_STEPS = 8


def from_behind(block, axis, distance):
    devices = range(lax.axis_size(axis))
    route = [((i - distance) % len(devices), i) for i in devices]
    return lax.ppermute(block, axis, route)


def fill(ref, count, value):
    def step(i, carry):
        ref[i] = value
        return carry

    lax.fori_loop(0, count, step, 0)


def invert_places(places, tile, index_ref, positions, stored):
    fill(index_ref, positions, -1)

    def step(n, carry):
        index_ref[places[tile[0], tile[1], n]] = n
        return carry

    lax.fori_loop(0, stored, step, 0)


def multiply_tiles(
    left_tile, right_tile, left_index, right_index, left_dense, right_column, emit, before=None,
    left_ready=None, right_ready=None,
):
    side = left_tile.shape[-1]
    zero_block = jnp.zeros((side, side), left_tile.dtype)
    right_column[...] = jnp.zeros(right_column.shape, right_column.dtype)
    if left_ready is not None:
        left_ready()

    def densify_left(r, carry):
        rows = pl.ds(pl.multiple_of(r * side, side), side)
        for k in range(KBLK):
            index = left_index[r * KBLK + k]
            block = left_tile[jnp.maximum(index, 0)]
            left_dense[rows, k * side:(k + 1) * side] = jnp.where(index >= 0, block, zero_block)
        return carry

    lax.fori_loop(0, ROWB, densify_left, 0)
    if right_ready is not None:
        right_ready()

    def place_column(cp, clear):
        for k in range(KBLK):
            for cc in range(COL_GROUP):
                index = right_index[k * COLB + cp * COL_GROUP + cc]

                @pl.when(index >= 0)
                def _():
                    block = zero_block if clear else right_tile[index]
                    right_column[k * side:(k + 1) * side, cc * side:(cc + 1) * side] = block

    def column_pair(cp, carry):
        if before is not None:
            before(cp)
        place_column(cp, False)

        def row_pair(rp, inner):
            rows = pl.ds(pl.multiple_of(rp * ROW_GROUP * side, ROW_GROUP * side), ROW_GROUP * side)
            result = jnp.dot(left_dense[rows, :], right_column[...], preferred_element_type=jnp.float32)
            emit(rp, cp, rows, result)
            return inner

        lax.fori_loop(0, ROWB // ROW_GROUP, row_pair, 0)
        place_column(cp, True)
        return carry

    lax.fori_loop(0, COLB // COL_GROUP, column_pair, 0)


def first_kernel(
    rows_grid, cols_grid, capacity,
    left_places, right_places, owners, left_tile, right_tile,
    partial, slot_of, left_index_next, right_index_next, outgoing,
    left_dense, right_column, left_index, right_index, counts, filled, zero_ref, zero_sems,
):
    side = left_tile.shape[-1]
    stored = left_tile.shape[0]
    row_here = lax.axis_index("row")
    col_here = lax.axis_index("col")
    row_next = lax.rem(row_here + 1, rows_grid)
    col_next = lax.rem(col_here + 1, cols_grid)
    invert_places(left_places, (row_here, col_here), left_index, ROWB * KBLK, stored)
    invert_places(right_places, (row_here, col_here), right_index, KBLK * COLB, stored)
    invert_places(left_places, (row_here, col_next), left_index_next, ROWB * KBLK, stored)
    invert_places(right_places, (row_next, col_here), right_index_next, KBLK * COLB, stored)
    fill(filled, filled.shape[0], 0)
    fill(counts, counts.shape[0], 0)

    def assign(m, carry):
        owner = owners[m]
        taken = counts[owner]
        slot = owner * capacity + taken
        slot_of[m] = slot
        filled[slot] = 1
        counts[owner] = taken + 1
        return carry

    lax.fori_loop(0, ROWB * COLB, assign, 0)
    zero_ref[...] = jnp.zeros(zero_ref.shape, zero_ref.dtype)

    def zero_slot(s, carry):
        @pl.when(filled[s] == 0)
        def _():
            pltpu.make_async_copy(zero_ref, outgoing.at[s], zero_sems.at[s]).start()

        return carry

    lax.fori_loop(0, outgoing.shape[0], zero_slot, 0)

    def emit(rp, cp, rows, result):
        partial[cp, rows, :] = result

    multiply_tiles(left_tile, right_tile, left_index, right_index, left_dense, right_column, emit)

    def wait_slot(s, carry):
        @pl.when(filled[s] == 0)
        def _():
            pltpu.make_async_copy(zero_ref, outgoing.at[s], zero_sems.at[s]).wait()

        return carry

    lax.fori_loop(0, outgoing.shape[0], wait_slot, 0)


def second_kernel(
    slot_of, left_index, right_index, left_tile, right_hbm, partial, outgoing,
    out,
    left_dense, right_column, partial_buf, staging, right_tile, partial_sems, out_sems, tile_sems,
):
    side = left_tile.shape[-1]
    pairs = COLB // COL_GROUP
    products = ROWB * COLB
    right_copy = pltpu.make_async_copy(right_hbm, right_tile, tile_sems.at[0])
    right_copy.start()

    def partial_copy(cp, buffer):
        return pltpu.make_async_copy(partial.at[cp], partial_buf.at[buffer], partial_sems.at[buffer])

    partial_copy(0, 0).start()

    def send_pair(cp):
        for r in range(ROWB):
            for cc in range(COL_GROUP):
                m = r * COLB + cp * COL_GROUP + cc
                pltpu.make_async_copy(staging.at[m], out.at[slot_of[m]], out_sems.at[m]).start()

    def before(cp):
        buffer = lax.rem(cp, 2)

        @pl.when(cp + 1 < pairs)
        def _():
            partial_copy(cp + 1, 1 - buffer).start()

        @pl.when(cp > 0)
        def _():
            send_pair(cp - 1)

        partial_copy(cp, buffer).wait()

    def emit(rp, cp, rows, result):
        buffer = lax.rem(cp, 2)
        total = result + partial_buf[buffer, rows, :]
        for rr in range(ROW_GROUP):
            for cc in range(COL_GROUP):
                m = (rp * ROW_GROUP + rr) * COLB + cp * COL_GROUP + cc
                piece = total[rr * side:(rr + 1) * side, cc * side:(cc + 1) * side]
                staging[m] = piece.astype(staging.dtype)

    multiply_tiles(
        left_tile, right_tile, left_index, right_index, left_dense, right_column, emit, before,
        None, right_copy.wait,
    )
    send_pair(pairs - 1)

    def wait_block(m, carry):
        pltpu.make_async_copy(staging.at[m], out.at[slot_of[m]], out_sems.at[m]).wait()
        return carry

    lax.fori_loop(0, products, wait_block, 0)


def pass_through(source, target):
    target[...] = source[...]


def body(left_values, left_places, right_values, right_places, owners):
    rows_grid = lax.axis_size("row")
    cols_grid = lax.axis_size("col")
    devices_all = rows_grid * cols_grid
    left_here = left_values[0, 0]
    right_here = right_values[0, 0]
    side = left_here.shape[-1]
    left_next = from_behind(left_here, "col", -1)
    right_next = from_behind(right_here, "row", -1)
    capacity = 2 * ROWB * COLB // devices_all
    slots = devices_all * capacity
    products = ROWB * COLB
    pairs = COLB // COL_GROUP
    smem = pl.BlockSpec(memory_space=pltpu.SMEM)
    vmem = pl.BlockSpec(memory_space=pltpu.VMEM)
    anywhere = pl.BlockSpec(memory_space=pl.ANY)
    work = [
        pltpu.VMEM((ROWB * side, KBLK * side), jnp.bfloat16),
        pltpu.VMEM((KBLK * side, COL_GROUP * side), jnp.bfloat16),
    ]
    flops = 2 * (ROWB * side) * (KBLK * side) * (COLB * side)
    tile_bytes = 2 * left_here.size * 2
    partial_bytes = ROWB * COLB * side * side * 4
    partial, slot_of, left_index, right_index, outgoing = pl.pallas_call(
        functools.partial(first_kernel, rows_grid, cols_grid, capacity),
        out_shape=(
            jax.ShapeDtypeStruct((pairs, ROWB * side, COL_GROUP * side), jnp.float32),
            jax.ShapeDtypeStruct((products,), jnp.int32),
            jax.ShapeDtypeStruct((ROWB * KBLK,), jnp.int32),
            jax.ShapeDtypeStruct((KBLK * COLB,), jnp.int32),
            jax.ShapeDtypeStruct((slots, side, side), jnp.bfloat16),
        ),
        in_specs=[smem, smem, smem, vmem, vmem],
        out_specs=(vmem, smem, smem, smem, anywhere),
        scratch_shapes=work + [
            pltpu.SMEM((ROWB * KBLK,), jnp.int32),
            pltpu.SMEM((KBLK * COLB,), jnp.int32),
            pltpu.SMEM((devices_all,), jnp.int32),
            pltpu.SMEM((slots,), jnp.int32),
            pltpu.VMEM((side, side), jnp.bfloat16),
            pltpu.SemaphoreType.DMA((slots,)),
        ],
        compiler_params=pltpu.CompilerParams(vmem_limit_bytes=60 * 1024 * 1024),
        cost_estimate=pl.CostEstimate(flops=flops, bytes_accessed=tile_bytes + partial_bytes, transcendentals=0),
    )(left_places, right_places, owners[0], left_here, right_here)
    outgoing = pl.pallas_call(
        second_kernel,
        out_shape=jax.ShapeDtypeStruct((slots, side, side), jnp.bfloat16),
        in_specs=[smem, smem, smem, vmem, anywhere, anywhere, anywhere],
        out_specs=anywhere,
        input_output_aliases={6: 0},
        scratch_shapes=work + [
            pltpu.VMEM((2, ROWB * side, COL_GROUP * side), jnp.float32),
            pltpu.VMEM((products, side, side), jnp.bfloat16),
            pltpu.VMEM(right_here.shape, right_here.dtype),
            pltpu.SemaphoreType.DMA((2,)),
            pltpu.SemaphoreType.DMA((products,)),
            pltpu.SemaphoreType.DMA((1,)),
        ],
        compiler_params=pltpu.CompilerParams(vmem_limit_bytes=60 * 1024 * 1024),
        cost_estimate=pl.CostEstimate(
            flops=flops, bytes_accessed=tile_bytes + partial_bytes + slots * side * side * 2, transcendentals=0
        ),
    )(slot_of, left_index, right_index, left_next, right_next, partial, outgoing)
    outgoing = outgoing.reshape(devices_all, capacity, side, side)
    received = lax.all_to_all(outgoing, ("row", "col"), split_axis=0, concat_axis=0, tiled=True)
    chunk = devices_all // COPY_STEPS
    block = pl.BlockSpec((chunk, capacity, side, side), lambda i: (i, 0, 0, 0))
    received = pl.pallas_call(
        pass_through,
        out_shape=jax.ShapeDtypeStruct(received.shape, received.dtype),
        grid=(COPY_STEPS,),
        in_specs=[block],
        out_specs=block,
        cost_estimate=pl.CostEstimate(flops=0, bytes_accessed=2 * received.size * 2, transcendentals=0),
    )(received)
    return received[None]


def solution(mesh):
    placed = (
        P("row", "col", None, None, None),
        P(),
        P("row", "col", None, None, None),
        P(),
        P(("row", "col"), None),
    )
    return jax.shard_map(
        body,
        mesh=mesh,
        in_specs=placed,
        out_specs=P(("row", "col"), None, None, None, None),
        check_vma=False,
    )
```

```python
import functools

import jax
import jax.numpy as jnp
from jax import lax
from jax.experimental import pallas as pl
from jax.experimental.pallas import tpu as pltpu
from jax.sharding import PartitionSpec as P

ROWB = 8
KBLK = 16
COLB = 16
COL_GROUP = 2
ROW_GROUP = 8
COPY_STEPS = 2


def from_behind(block, axis, distance):
    devices = range(lax.axis_size(axis))
    route = [((i - distance) % len(devices), i) for i in devices]
    return lax.ppermute(block, axis, route)


def fill(ref, count, value):
    def step(i, carry):
        ref[i] = value
        return carry

    lax.fori_loop(0, count, step, 0)


def invert_places(places, tile, index_ref, positions, stored):
    fill(index_ref, positions, -1)

    def step(n, carry):
        index_ref[places[tile[0], tile[1], n]] = n
        return carry

    lax.fori_loop(0, stored, step, 0)


def multiply_tiles(
    left_tile, right_tile, left_index, right_index, left_dense, right_column, emit, before=None,
    left_ready=None, right_ready=None,
):
    side = left_tile.shape[-1]
    zero_block = jnp.zeros((side, side), left_tile.dtype)
    right_column[...] = jnp.zeros(right_column.shape, right_column.dtype)
    if left_ready is not None:
        left_ready()

    def densify_left(r, carry):
        rows = pl.ds(pl.multiple_of(r * side, side), side)
        for k in range(KBLK):
            index = left_index[r * KBLK + k]
            block = left_tile[jnp.maximum(index, 0)]
            left_dense[rows, k * side:(k + 1) * side] = jnp.where(index >= 0, block, zero_block)
        return carry

    lax.fori_loop(0, ROWB, densify_left, 0)
    if right_ready is not None:
        right_ready()

    def place_column(cp, clear):
        for k in range(KBLK):
            for cc in range(COL_GROUP):
                index = right_index[k * COLB + cp * COL_GROUP + cc]

                @pl.when(index >= 0)
                def _():
                    block = zero_block if clear else right_tile[index]
                    right_column[k * side:(k + 1) * side, cc * side:(cc + 1) * side] = block

    def column_pair(cp, carry):
        if before is not None:
            before(cp)
        place_column(cp, False)

        def row_pair(rp, inner):
            rows = pl.ds(pl.multiple_of(rp * ROW_GROUP * side, ROW_GROUP * side), ROW_GROUP * side)
            result = jnp.dot(left_dense[rows, :], right_column[...], preferred_element_type=jnp.float32)
            emit(rp, cp, rows, result)
            return inner

        lax.fori_loop(0, ROWB // ROW_GROUP, row_pair, 0)
        place_column(cp, True)
        return carry

    lax.fori_loop(0, COLB // COL_GROUP, column_pair, 0)


def first_kernel(
    rows_grid, cols_grid, capacity,
    left_places, right_places, owners, left_tile, right_tile,
    partial, slot_of, left_index_next, right_index_next, outgoing,
    left_dense, right_column, left_index, right_index, counts, filled, zero_ref, zero_sems,
):
    side = left_tile.shape[-1]
    stored = left_tile.shape[0]
    row_here = lax.axis_index("row")
    col_here = lax.axis_index("col")
    row_next = lax.rem(row_here + 1, rows_grid)
    col_next = lax.rem(col_here + 1, cols_grid)
    invert_places(left_places, (row_here, col_here), left_index, ROWB * KBLK, stored)
    invert_places(right_places, (row_here, col_here), right_index, KBLK * COLB, stored)
    invert_places(left_places, (row_here, col_next), left_index_next, ROWB * KBLK, stored)
    invert_places(right_places, (row_next, col_here), right_index_next, KBLK * COLB, stored)
    fill(filled, filled.shape[0], 0)
    fill(counts, counts.shape[0], 0)

    def assign(m, carry):
        owner = owners[m]
        taken = counts[owner]
        slot = owner * capacity + taken
        slot_of[m] = slot
        filled[slot] = 1
        counts[owner] = taken + 1
        return carry

    lax.fori_loop(0, ROWB * COLB, assign, 0)
    zero_ref[...] = jnp.zeros(zero_ref.shape, zero_ref.dtype)

    def zero_slot(s, carry):
        @pl.when(filled[s] == 0)
        def _():
            pltpu.make_async_copy(zero_ref, outgoing.at[s], zero_sems.at[s]).start()

        return carry

    lax.fori_loop(0, outgoing.shape[0], zero_slot, 0)

    def emit(rp, cp, rows, result):
        partial[cp, rows, :] = result

    multiply_tiles(left_tile, right_tile, left_index, right_index, left_dense, right_column, emit)

    def wait_slot(s, carry):
        @pl.when(filled[s] == 0)
        def _():
            pltpu.make_async_copy(zero_ref, outgoing.at[s], zero_sems.at[s]).wait()

        return carry

    lax.fori_loop(0, outgoing.shape[0], wait_slot, 0)


def second_kernel(
    slot_of, left_index, right_index, left_tile, right_hbm, partial, outgoing,
    out,
    left_dense, right_column, partial_buf, staging, right_tile, partial_sems, out_sems, tile_sems,
):
    side = left_tile.shape[-1]
    pairs = COLB // COL_GROUP
    products = ROWB * COLB
    right_copy = pltpu.make_async_copy(right_hbm, right_tile, tile_sems.at[0])
    right_copy.start()

    def partial_copy(cp, buffer):
        return pltpu.make_async_copy(partial.at[cp], partial_buf.at[buffer], partial_sems.at[buffer])

    partial_copy(0, 0).start()

    def send_pair(cp):
        for r in range(ROWB):
            for cc in range(COL_GROUP):
                m = r * COLB + cp * COL_GROUP + cc
                pltpu.make_async_copy(staging.at[m], out.at[slot_of[m]], out_sems.at[m]).start()

    def before(cp):
        buffer = lax.rem(cp, 2)

        @pl.when(cp + 1 < pairs)
        def _():
            partial_copy(cp + 1, 1 - buffer).start()

        @pl.when(cp > 0)
        def _():
            send_pair(cp - 1)

        partial_copy(cp, buffer).wait()

    def emit(rp, cp, rows, result):
        buffer = lax.rem(cp, 2)
        total = result + partial_buf[buffer, rows, :]
        for rr in range(ROW_GROUP):
            for cc in range(COL_GROUP):
                m = (rp * ROW_GROUP + rr) * COLB + cp * COL_GROUP + cc
                piece = total[rr * side:(rr + 1) * side, cc * side:(cc + 1) * side]
                staging[m] = piece.astype(staging.dtype)

    multiply_tiles(
        left_tile, right_tile, left_index, right_index, left_dense, right_column, emit, before,
        None, right_copy.wait,
    )
    send_pair(pairs - 1)

    def wait_block(m, carry):
        pltpu.make_async_copy(staging.at[m], out.at[slot_of[m]], out_sems.at[m]).wait()
        return carry

    lax.fori_loop(0, products, wait_block, 0)


def pass_through(source, target):
    target[...] = source[...]


def body(left_values, left_places, right_values, right_places, owners):
    rows_grid = lax.axis_size("row")
    cols_grid = lax.axis_size("col")
    devices_all = rows_grid * cols_grid
    left_here = left_values[0, 0]
    right_here = right_values[0, 0]
    side = left_here.shape[-1]
    left_next = from_behind(left_here, "col", -1)
    right_next = from_behind(right_here, "row", -1)
    capacity = 2 * ROWB * COLB // devices_all
    slots = devices_all * capacity
    products = ROWB * COLB
    pairs = COLB // COL_GROUP
    smem = pl.BlockSpec(memory_space=pltpu.SMEM)
    vmem = pl.BlockSpec(memory_space=pltpu.VMEM)
    anywhere = pl.BlockSpec(memory_space=pl.ANY)
    work = [
        pltpu.VMEM((ROWB * side, KBLK * side), jnp.bfloat16),
        pltpu.VMEM((KBLK * side, COL_GROUP * side), jnp.bfloat16),
    ]
    flops = 2 * (ROWB * side) * (KBLK * side) * (COLB * side)
    tile_bytes = 2 * left_here.size * 2
    partial_bytes = ROWB * COLB * side * side * 4
    partial, slot_of, left_index, right_index, outgoing = pl.pallas_call(
        functools.partial(first_kernel, rows_grid, cols_grid, capacity),
        out_shape=(
            jax.ShapeDtypeStruct((pairs, ROWB * side, COL_GROUP * side), jnp.float32),
            jax.ShapeDtypeStruct((products,), jnp.int32),
            jax.ShapeDtypeStruct((ROWB * KBLK,), jnp.int32),
            jax.ShapeDtypeStruct((KBLK * COLB,), jnp.int32),
            jax.ShapeDtypeStruct((slots, side, side), jnp.bfloat16),
        ),
        in_specs=[smem, smem, smem, vmem, vmem],
        out_specs=(vmem, smem, smem, smem, anywhere),
        scratch_shapes=work + [
            pltpu.SMEM((ROWB * KBLK,), jnp.int32),
            pltpu.SMEM((KBLK * COLB,), jnp.int32),
            pltpu.SMEM((devices_all,), jnp.int32),
            pltpu.SMEM((slots,), jnp.int32),
            pltpu.VMEM((side, side), jnp.bfloat16),
            pltpu.SemaphoreType.DMA((slots,)),
        ],
        compiler_params=pltpu.CompilerParams(vmem_limit_bytes=60 * 1024 * 1024),
        cost_estimate=pl.CostEstimate(flops=flops, bytes_accessed=tile_bytes + partial_bytes, transcendentals=0),
    )(left_places, right_places, owners[0], left_here, right_here)
    outgoing = pl.pallas_call(
        second_kernel,
        out_shape=jax.ShapeDtypeStruct((slots, side, side), jnp.bfloat16),
        in_specs=[smem, smem, smem, vmem, anywhere, anywhere, anywhere],
        out_specs=anywhere,
        input_output_aliases={6: 0},
        scratch_shapes=work + [
            pltpu.VMEM((2, ROWB * side, COL_GROUP * side), jnp.float32),
            pltpu.VMEM((products, side, side), jnp.bfloat16),
            pltpu.VMEM(right_here.shape, right_here.dtype),
            pltpu.SemaphoreType.DMA((2,)),
            pltpu.SemaphoreType.DMA((products,)),
            pltpu.SemaphoreType.DMA((1,)),
        ],
        compiler_params=pltpu.CompilerParams(vmem_limit_bytes=60 * 1024 * 1024),
        cost_estimate=pl.CostEstimate(
            flops=flops, bytes_accessed=tile_bytes + partial_bytes + slots * side * side * 2, transcendentals=0
        ),
    )(slot_of, left_index, right_index, left_next, right_next, partial, outgoing)
    outgoing = outgoing.reshape(devices_all, capacity, side, side)
    received = lax.all_to_all(outgoing, ("row", "col"), split_axis=0, concat_axis=0, tiled=True)
    chunk = devices_all // COPY_STEPS
    block = pl.BlockSpec((chunk, capacity, side, side), lambda i: (i, 0, 0, 0))
    received = pl.pallas_call(
        pass_through,
        out_shape=jax.ShapeDtypeStruct(received.shape, received.dtype),
        grid=(COPY_STEPS,),
        in_specs=[block],
        out_specs=block,
        cost_estimate=pl.CostEstimate(flops=0, bytes_accessed=2 * received.size * 2, transcendentals=0),
    )(received)
    return received[None]


def solution(mesh):
    placed = (
        P("row", "col", None, None, None),
        P(),
        P("row", "col", None, None, None),
        P(),
        P(("row", "col"), None),
    )
    return jax.shard_map(
        body,
        mesh=mesh,
        in_specs=placed,
        out_specs=P(("row", "col"), None, None, None, None),
        check_vma=False,
    )
```

```python
import functools

import jax
import jax.numpy as jnp
from jax import lax
from jax.experimental import pallas as pl
from jax.experimental.pallas import tpu as pltpu
from jax.sharding import PartitionSpec as P

ROWB = 8
KBLK = 16
COLB = 16
COL_GROUP = 2
ROW_GROUP = 8
COPY_STEPS = 2


def from_behind(block, axis, distance):
    devices = range(lax.axis_size(axis))
    route = [((i - distance) % len(devices), i) for i in devices]
    return lax.ppermute(block, axis, route)


def fill(ref, count, value):
    def step(i, carry):
        ref[i] = value
        return carry

    lax.fori_loop(0, count, step, 0)


def invert_places(places, tile, index_ref, positions, stored):
    fill(index_ref, positions, -1)

    def step(n, carry):
        index_ref[places[tile[0], tile[1], n]] = n
        return carry

    lax.fori_loop(0, stored, step, 0)


def multiply_tiles(
    left_tile, right_tile, left_index, right_index, left_dense, right_column, emit, before=None,
    left_ready=None, right_ready=None, column_of=None,
):
    side = left_tile.shape[-1]
    zero_block = jnp.zeros((side, side), left_tile.dtype)
    if column_of is None:
        right_column[...] = jnp.zeros(right_column.shape, right_column.dtype)
    if left_ready is not None:
        left_ready()

    def densify_left(r, carry):
        rows = pl.ds(pl.multiple_of(r * side, side), side)
        for k in range(KBLK):
            index = left_index[r * KBLK + k]
            block = left_tile[jnp.maximum(index, 0)]
            left_dense[rows, k * side:(k + 1) * side] = jnp.where(index >= 0, block, zero_block)
        return carry

    lax.fori_loop(0, ROWB, densify_left, 0)
    if right_ready is not None:
        right_ready()

    def place_column(cp, clear):
        for k in range(KBLK):
            for cc in range(COL_GROUP):
                index = right_index[k * COLB + cp * COL_GROUP + cc]

                @pl.when(index >= 0)
                def _():
                    block = zero_block if clear else right_tile[index]
                    right_column[k * side:(k + 1) * side, cc * side:(cc + 1) * side] = block

    def column_pair(cp, carry):
        if before is not None:
            before(cp)
        if column_of is None:
            place_column(cp, False)
            column = right_column
        else:
            column = column_of(cp)

        def row_pair(rp, inner):
            rows = pl.ds(pl.multiple_of(rp * ROW_GROUP * side, ROW_GROUP * side), ROW_GROUP * side)
            result = jnp.dot(left_dense[rows, :], column[...], preferred_element_type=jnp.float32)
            emit(rp, cp, rows, result)
            return inner

        lax.fori_loop(0, ROWB // ROW_GROUP, row_pair, 0)
        if column_of is None:
            place_column(cp, True)
        return carry

    lax.fori_loop(0, COLB // COL_GROUP, column_pair, 0)


def first_kernel(
    rows_grid, cols_grid, capacity,
    left_places, right_places, owners, left_tile, right_tile,
    partial, slot_of, left_index_next, right_index_next, outgoing,
    left_dense, right_column, left_index, right_index, counts, filled, zero_ref, zero_sems,
):
    side = left_tile.shape[-1]
    stored = left_tile.shape[0]
    row_here = lax.axis_index("row")
    col_here = lax.axis_index("col")
    row_next = lax.rem(row_here + 1, rows_grid)
    col_next = lax.rem(col_here + 1, cols_grid)
    invert_places(left_places, (row_here, col_here), left_index, ROWB * KBLK, stored)
    invert_places(right_places, (row_here, col_here), right_index, KBLK * COLB, stored)
    invert_places(left_places, (row_here, col_next), left_index_next, ROWB * KBLK, stored)
    invert_places(right_places, (row_next, col_here), right_index_next, KBLK * COLB, stored)
    fill(filled, filled.shape[0], 0)
    fill(counts, counts.shape[0], 0)

    def assign(m, carry):
        owner = owners[m]
        taken = counts[owner]
        slot = owner * capacity + taken
        slot_of[m] = slot
        filled[slot] = 1
        counts[owner] = taken + 1
        return carry

    lax.fori_loop(0, ROWB * COLB, assign, 0)
    zero_ref[...] = jnp.zeros(zero_ref.shape, zero_ref.dtype)

    def zero_slot(s, carry):
        @pl.when(filled[s] == 0)
        def _():
            pltpu.make_async_copy(zero_ref, outgoing.at[s], zero_sems.at[s]).start()

        return carry

    lax.fori_loop(0, outgoing.shape[0], zero_slot, 0)

    def emit(rp, cp, rows, result):
        partial[cp, rows, :] = result

    multiply_tiles(left_tile, right_tile, left_index, right_index, left_dense, right_column, emit)

    def wait_slot(s, carry):
        @pl.when(filled[s] == 0)
        def _():
            pltpu.make_async_copy(zero_ref, outgoing.at[s], zero_sems.at[s]).wait()

        return carry

    lax.fori_loop(0, outgoing.shape[0], wait_slot, 0)


def column_kernel(right_index, right_tile, columns, column_buf, sems):
    side = right_tile.shape[-1]
    pairs = COLB // COL_GROUP
    zero_block = jnp.zeros((side, side), right_tile.dtype)

    def send(cp, buffer):
        return pltpu.make_async_copy(column_buf.at[buffer], columns.at[cp], sems.at[buffer])

    def column_pair(cp, carry):
        buffer = lax.rem(cp, 2)

        @pl.when(cp >= 2)
        def _():
            send(cp - 2, buffer).wait()

        for k in range(KBLK):
            for cc in range(COL_GROUP):
                index = right_index[k * COLB + cp * COL_GROUP + cc]
                block = right_tile[jnp.maximum(index, 0)]
                column_buf[buffer, k * side:(k + 1) * side, cc * side:(cc + 1) * side] = jnp.where(
                    index >= 0, block, zero_block
                )
        send(cp, buffer).start()
        return carry

    lax.fori_loop(0, pairs, column_pair, 0)
    send(pairs - 2, 0).wait()
    send(pairs - 1, 1).wait()


def second_kernel(
    slot_of, left_index, left_tile, columns, partial, outgoing,
    out,
    left_dense, column_buf, partial_buf, staging, partial_sems, column_sems, out_sems,
):
    side = left_tile.shape[-1]
    pairs = COLB // COL_GROUP
    products = ROWB * COLB

    def partial_copy(cp, buffer):
        return pltpu.make_async_copy(partial.at[cp], partial_buf.at[buffer], partial_sems.at[buffer])

    def column_copy(cp, buffer):
        return pltpu.make_async_copy(columns.at[cp], column_buf.at[buffer], column_sems.at[buffer])

    partial_copy(0, 0).start()
    column_copy(0, 0).start()

    def send_pair(cp):
        for r in range(ROWB):
            for cc in range(COL_GROUP):
                m = r * COLB + cp * COL_GROUP + cc
                pltpu.make_async_copy(staging.at[m], out.at[slot_of[m]], out_sems.at[m]).start()

    def before(cp):
        buffer = lax.rem(cp, 2)

        @pl.when(cp + 1 < pairs)
        def _():
            partial_copy(cp + 1, 1 - buffer).start()
            column_copy(cp + 1, 1 - buffer).start()

        @pl.when(cp > 0)
        def _():
            send_pair(cp - 1)

        partial_copy(cp, buffer).wait()
        column_copy(cp, buffer).wait()

    def emit(rp, cp, rows, result):
        buffer = lax.rem(cp, 2)
        total = result + partial_buf[buffer, rows, :]
        for rr in range(ROW_GROUP):
            for cc in range(COL_GROUP):
                m = (rp * ROW_GROUP + rr) * COLB + cp * COL_GROUP + cc
                piece = total[rr * side:(rr + 1) * side, cc * side:(cc + 1) * side]
                staging[m] = piece.astype(staging.dtype)

    multiply_tiles(
        left_tile, None, left_index, None, left_dense, None, emit, before,
        column_of=lambda cp: column_buf.at[lax.rem(cp, 2)],
    )
    send_pair(pairs - 1)

    def wait_block(m, carry):
        pltpu.make_async_copy(staging.at[m], out.at[slot_of[m]], out_sems.at[m]).wait()
        return carry

    lax.fori_loop(0, products, wait_block, 0)


def pass_through(source, target):
    target[...] = source[...]


def body(left_values, left_places, right_values, right_places, owners):
    rows_grid = lax.axis_size("row")
    cols_grid = lax.axis_size("col")
    devices_all = rows_grid * cols_grid
    left_here = left_values[0, 0]
    right_here = right_values[0, 0]
    side = left_here.shape[-1]
    left_next = from_behind(left_here, "col", -1)
    right_next = from_behind(right_here, "row", -1)
    capacity = 2 * ROWB * COLB // devices_all
    slots = devices_all * capacity
    products = ROWB * COLB
    pairs = COLB // COL_GROUP
    smem = pl.BlockSpec(memory_space=pltpu.SMEM)
    vmem = pl.BlockSpec(memory_space=pltpu.VMEM)
    anywhere = pl.BlockSpec(memory_space=pl.ANY)
    work = [
        pltpu.VMEM((ROWB * side, KBLK * side), jnp.bfloat16),
        pltpu.VMEM((KBLK * side, COL_GROUP * side), jnp.bfloat16),
    ]
    flops = 2 * (ROWB * side) * (KBLK * side) * (COLB * side)
    tile_bytes = 2 * left_here.size * 2
    partial_bytes = ROWB * COLB * side * side * 4
    partial, slot_of, left_index, right_index, outgoing = pl.pallas_call(
        functools.partial(first_kernel, rows_grid, cols_grid, capacity),
        out_shape=(
            jax.ShapeDtypeStruct((pairs, ROWB * side, COL_GROUP * side), jnp.float32),
            jax.ShapeDtypeStruct((products,), jnp.int32),
            jax.ShapeDtypeStruct((ROWB * KBLK,), jnp.int32),
            jax.ShapeDtypeStruct((KBLK * COLB,), jnp.int32),
            jax.ShapeDtypeStruct((slots, side, side), jnp.bfloat16),
        ),
        in_specs=[smem, smem, smem, vmem, vmem],
        out_specs=(vmem, smem, smem, smem, anywhere),
        scratch_shapes=work + [
            pltpu.SMEM((ROWB * KBLK,), jnp.int32),
            pltpu.SMEM((KBLK * COLB,), jnp.int32),
            pltpu.SMEM((devices_all,), jnp.int32),
            pltpu.SMEM((slots,), jnp.int32),
            pltpu.VMEM((side, side), jnp.bfloat16),
            pltpu.SemaphoreType.DMA((slots,)),
        ],
        compiler_params=pltpu.CompilerParams(vmem_limit_bytes=60 * 1024 * 1024),
        cost_estimate=pl.CostEstimate(flops=flops, bytes_accessed=tile_bytes + partial_bytes, transcendentals=0),
    )(left_places, right_places, owners[0], left_here, right_here)
    column_bytes = pairs * KBLK * side * COL_GROUP * side * 2
    columns = pl.pallas_call(
        column_kernel,
        out_shape=jax.ShapeDtypeStruct((pairs, KBLK * side, COL_GROUP * side), jnp.bfloat16),
        in_specs=[smem, vmem],
        out_specs=anywhere,
        scratch_shapes=[
            pltpu.VMEM((2, KBLK * side, COL_GROUP * side), jnp.bfloat16),
            pltpu.SemaphoreType.DMA((2,)),
        ],
        cost_estimate=pl.CostEstimate(flops=0, bytes_accessed=left_here.size * 2 + column_bytes, transcendentals=0),
    )(right_index, right_next)
    outgoing = pl.pallas_call(
        second_kernel,
        out_shape=jax.ShapeDtypeStruct((slots, side, side), jnp.bfloat16),
        in_specs=[smem, smem, vmem, anywhere, anywhere, anywhere],
        out_specs=anywhere,
        input_output_aliases={5: 0},
        scratch_shapes=[
            pltpu.VMEM((ROWB * side, KBLK * side), jnp.bfloat16),
            pltpu.VMEM((2, KBLK * side, COL_GROUP * side), jnp.bfloat16),
            pltpu.VMEM((2, ROWB * side, COL_GROUP * side), jnp.float32),
            pltpu.VMEM((products, side, side), jnp.bfloat16),
            pltpu.SemaphoreType.DMA((2,)),
            pltpu.SemaphoreType.DMA((2,)),
            pltpu.SemaphoreType.DMA((products,)),
        ],
        compiler_params=pltpu.CompilerParams(vmem_limit_bytes=60 * 1024 * 1024),
        cost_estimate=pl.CostEstimate(
            flops=flops, bytes_accessed=tile_bytes + partial_bytes + slots * side * side * 2, transcendentals=0
        ),
    )(slot_of, left_index, left_next, columns, partial, outgoing)
    outgoing = outgoing.reshape(devices_all, capacity, side, side)
    received = lax.all_to_all(outgoing, ("row", "col"), split_axis=0, concat_axis=0, tiled=True)
    chunk = devices_all // COPY_STEPS
    block = pl.BlockSpec((chunk, capacity, side, side), lambda i: (i, 0, 0, 0))
    received = pl.pallas_call(
        pass_through,
        out_shape=jax.ShapeDtypeStruct(received.shape, received.dtype),
        grid=(COPY_STEPS,),
        in_specs=[block],
        out_specs=block,
        cost_estimate=pl.CostEstimate(flops=0, bytes_accessed=2 * received.size * 2, transcendentals=0),
    )(received)
    return received[None]


def solution(mesh):
    placed = (
        P("row", "col", None, None, None),
        P(),
        P("row", "col", None, None, None),
        P(),
        P(("row", "col"), None),
    )
    return jax.shard_map(
        body,
        mesh=mesh,
        in_specs=placed,
        out_specs=P(("row", "col"), None, None, None, None),
        check_vma=False,
    )
```

```python
import functools

import jax
import jax.numpy as jnp
from jax import lax
from jax.experimental import pallas as pl
from jax.experimental.pallas import tpu as pltpu
from jax.sharding import PartitionSpec as P

ROWB = 8
KBLK = 16
COLB = 16
COL_GROUP = 2
ROW_GROUP = 8
COPY_STEPS = 2


def from_behind(block, axis, distance):
    devices = range(lax.axis_size(axis))
    route = [((i - distance) % len(devices), i) for i in devices]
    return lax.ppermute(block, axis, route)


def fill(ref, count, value):
    def step(i, carry):
        ref[i] = value
        return carry

    lax.fori_loop(0, count, step, 0)


def invert_places(places, tile, index_ref, positions, stored):
    fill(index_ref, positions, -1)

    def step(n, carry):
        index_ref[places[tile[0], tile[1], n]] = n
        return carry

    lax.fori_loop(0, stored, step, 0)


def multiply_tiles(
    left_tile, right_tile, left_index, right_index, left_dense, right_column, emit, before=None,
    left_ready=None, right_ready=None, column_of=None,
):
    side = left_tile.shape[-1]
    zero_block = jnp.zeros((side, side), left_tile.dtype)
    if left_ready is not None:
        left_ready()

    def densify_left(r, carry):
        rows = pl.ds(pl.multiple_of(r * side, side), side)
        for k in range(KBLK):
            index = left_index[r * KBLK + k]
            block = left_tile[jnp.maximum(index, 0)]
            left_dense[rows, k * side:(k + 1) * side] = jnp.where(index >= 0, block, zero_block)
        return carry

    lax.fori_loop(0, ROWB, densify_left, 0)
    if right_ready is not None:
        right_ready()

    def place_column(cp, clear):
        if clear:
            return
        for k in range(KBLK):
            for cc in range(COL_GROUP):
                index = right_index[k * COLB + cp * COL_GROUP + cc]
                block = right_tile[jnp.maximum(index, 0)]
                right_column[k * side:(k + 1) * side, cc * side:(cc + 1) * side] = jnp.where(
                    index >= 0, block, zero_block
                )

    def column_pair(cp, carry):
        if before is not None:
            before(cp)
        if column_of is None:
            place_column(cp, False)
            column = right_column
        else:
            column = column_of(cp)

        def row_pair(rp, inner):
            rows = pl.ds(pl.multiple_of(rp * ROW_GROUP * side, ROW_GROUP * side), ROW_GROUP * side)
            result = jnp.dot(left_dense[rows, :], column[...], preferred_element_type=jnp.float32)
            emit(rp, cp, rows, result)
            return inner

        lax.fori_loop(0, ROWB // ROW_GROUP, row_pair, 0)
        if column_of is None:
            place_column(cp, True)
        return carry

    lax.fori_loop(0, COLB // COL_GROUP, column_pair, 0)


def first_kernel(
    rows_grid, cols_grid, capacity,
    left_places, right_places, owners, left_tile, right_tile,
    partial, slot_of, left_index_next, right_index_next, outgoing,
    left_dense, right_column, left_index, right_index, counts, filled, zero_ref, zero_sems,
):
    side = left_tile.shape[-1]
    stored = left_tile.shape[0]
    row_here = lax.axis_index("row")
    col_here = lax.axis_index("col")
    row_next = lax.rem(row_here + 1, rows_grid)
    col_next = lax.rem(col_here + 1, cols_grid)
    invert_places(left_places, (row_here, col_here), left_index, ROWB * KBLK, stored)
    invert_places(right_places, (row_here, col_here), right_index, KBLK * COLB, stored)
    invert_places(left_places, (row_here, col_next), left_index_next, ROWB * KBLK, stored)
    invert_places(right_places, (row_next, col_here), right_index_next, KBLK * COLB, stored)
    fill(filled, filled.shape[0], 0)
    fill(counts, counts.shape[0], 0)

    def assign(m, carry):
        owner = owners[m]
        taken = counts[owner]
        slot = owner * capacity + taken
        slot_of[m] = slot
        filled[slot] = 1
        counts[owner] = taken + 1
        return carry

    lax.fori_loop(0, ROWB * COLB, assign, 0)
    zero_ref[...] = jnp.zeros(zero_ref.shape, zero_ref.dtype)

    def zero_slot(s, carry):
        @pl.when(filled[s] == 0)
        def _():
            pltpu.make_async_copy(zero_ref, outgoing.at[s], zero_sems.at[0]).start()

        return carry

    lax.fori_loop(0, outgoing.shape[0], zero_slot, 0)

    def emit(rp, cp, rows, result):
        partial[cp, rows, :] = result

    multiply_tiles(left_tile, right_tile, left_index, right_index, left_dense, right_column, emit)

    unfilled = outgoing.shape[0] - ROWB * COLB
    pltpu.make_async_copy(outgoing.at[pl.ds(0, unfilled)], outgoing.at[pl.ds(0, unfilled)], zero_sems.at[0]).wait()


def column_kernel(right_index, right_tile, columns, column_buf, sems):
    side = right_tile.shape[-1]
    pairs = COLB // COL_GROUP
    zero_block = jnp.zeros((side, side), right_tile.dtype)

    def send(cp, buffer):
        return pltpu.make_async_copy(column_buf.at[buffer], columns.at[cp], sems.at[buffer])

    def column_pair(cp, carry):
        buffer = lax.rem(cp, 2)

        @pl.when(cp >= 2)
        def _():
            send(cp - 2, buffer).wait()

        for k in range(KBLK):
            for cc in range(COL_GROUP):
                index = right_index[k * COLB + cp * COL_GROUP + cc]
                block = right_tile[jnp.maximum(index, 0)]
                column_buf[buffer, k * side:(k + 1) * side, cc * side:(cc + 1) * side] = jnp.where(
                    index >= 0, block, zero_block
                )
        send(cp, buffer).start()
        return carry

    lax.fori_loop(0, pairs, column_pair, 0)
    send(pairs - 2, 0).wait()
    send(pairs - 1, 1).wait()


def second_kernel(
    slot_of, left_index, left_tile, columns, partial, outgoing,
    out,
    left_dense, column_buf, partial_buf, staging, partial_sems, column_sems, out_sems,
):
    side = left_tile.shape[-1]
    pairs = COLB // COL_GROUP
    products = ROWB * COLB

    def partial_copy(cp, buffer):
        return pltpu.make_async_copy(partial.at[cp], partial_buf.at[buffer], partial_sems.at[buffer])

    def column_copy(cp, buffer):
        return pltpu.make_async_copy(columns.at[cp], column_buf.at[buffer], column_sems.at[buffer])

    partial_copy(0, 0).start()
    column_copy(0, 0).start()

    def send_pair(cp):
        for r in range(ROWB):
            for cc in range(COL_GROUP):
                m = r * COLB + cp * COL_GROUP + cc
                pltpu.make_async_copy(staging.at[m], out.at[slot_of[m]], out_sems.at[0]).start()

    def before(cp):
        buffer = lax.rem(cp, 2)

        @pl.when(cp + 1 < pairs)
        def _():
            partial_copy(cp + 1, 1 - buffer).start()
            column_copy(cp + 1, 1 - buffer).start()

        @pl.when(cp > 0)
        def _():
            send_pair(cp - 1)

        partial_copy(cp, buffer).wait()
        column_copy(cp, buffer).wait()

    def emit(rp, cp, rows, result):
        buffer = lax.rem(cp, 2)
        total = result + partial_buf[buffer, rows, :]
        for rr in range(ROW_GROUP):
            for cc in range(COL_GROUP):
                m = (rp * ROW_GROUP + rr) * COLB + cp * COL_GROUP + cc
                piece = total[rr * side:(rr + 1) * side, cc * side:(cc + 1) * side]
                staging[m] = piece.astype(staging.dtype)

    multiply_tiles(
        left_tile, None, left_index, None, left_dense, None, emit, before,
        column_of=lambda cp: column_buf.at[lax.rem(cp, 2)],
    )
    send_pair(pairs - 1)

    pltpu.make_async_copy(staging, out.at[pl.ds(0, products)], out_sems.at[0]).wait()


def pass_through(source, target):
    target[...] = source[...]


def body(left_values, left_places, right_values, right_places, owners):
    rows_grid = lax.axis_size("row")
    cols_grid = lax.axis_size("col")
    devices_all = rows_grid * cols_grid
    left_here = left_values[0, 0]
    right_here = right_values[0, 0]
    side = left_here.shape[-1]
    left_next = from_behind(left_here, "col", -1)
    right_next = from_behind(right_here, "row", -1)
    capacity = 2 * ROWB * COLB // devices_all
    slots = devices_all * capacity
    products = ROWB * COLB
    pairs = COLB // COL_GROUP
    smem = pl.BlockSpec(memory_space=pltpu.SMEM)
    vmem = pl.BlockSpec(memory_space=pltpu.VMEM)
    anywhere = pl.BlockSpec(memory_space=pl.ANY)
    work = [
        pltpu.VMEM((ROWB * side, KBLK * side), jnp.bfloat16),
        pltpu.VMEM((KBLK * side, COL_GROUP * side), jnp.bfloat16),
    ]
    flops = 2 * (ROWB * side) * (KBLK * side) * (COLB * side)
    tile_bytes = 2 * left_here.size * 2
    partial_bytes = ROWB * COLB * side * side * 4
    partial, slot_of, left_index, right_index, outgoing = pl.pallas_call(
        functools.partial(first_kernel, rows_grid, cols_grid, capacity),
        out_shape=(
            jax.ShapeDtypeStruct((pairs, ROWB * side, COL_GROUP * side), jnp.float32),
            jax.ShapeDtypeStruct((products,), jnp.int32),
            jax.ShapeDtypeStruct((ROWB * KBLK,), jnp.int32),
            jax.ShapeDtypeStruct((KBLK * COLB,), jnp.int32),
            jax.ShapeDtypeStruct((slots, side, side), jnp.bfloat16),
        ),
        in_specs=[smem, smem, smem, vmem, vmem],
        out_specs=(vmem, smem, smem, smem, anywhere),
        scratch_shapes=work + [
            pltpu.SMEM((ROWB * KBLK,), jnp.int32),
            pltpu.SMEM((KBLK * COLB,), jnp.int32),
            pltpu.SMEM((devices_all,), jnp.int32),
            pltpu.SMEM((slots,), jnp.int32),
            pltpu.VMEM((side, side), jnp.bfloat16),
            pltpu.SemaphoreType.DMA((1,)),
        ],
        compiler_params=pltpu.CompilerParams(vmem_limit_bytes=60 * 1024 * 1024),
        cost_estimate=pl.CostEstimate(flops=flops, bytes_accessed=tile_bytes + partial_bytes, transcendentals=0),
    )(left_places, right_places, owners[0], left_here, right_here)
    column_bytes = pairs * KBLK * side * COL_GROUP * side * 2
    columns = pl.pallas_call(
        column_kernel,
        out_shape=jax.ShapeDtypeStruct((pairs, KBLK * side, COL_GROUP * side), jnp.bfloat16),
        in_specs=[smem, vmem],
        out_specs=anywhere,
        scratch_shapes=[
            pltpu.VMEM((2, KBLK * side, COL_GROUP * side), jnp.bfloat16),
            pltpu.SemaphoreType.DMA((2,)),
        ],
        cost_estimate=pl.CostEstimate(flops=0, bytes_accessed=left_here.size * 2 + column_bytes, transcendentals=0),
    )(right_index, right_next)
    outgoing = pl.pallas_call(
        second_kernel,
        out_shape=jax.ShapeDtypeStruct((slots, side, side), jnp.bfloat16),
        in_specs=[smem, smem, vmem, anywhere, anywhere, anywhere],
        out_specs=anywhere,
        input_output_aliases={5: 0},
        scratch_shapes=[
            pltpu.VMEM((ROWB * side, KBLK * side), jnp.bfloat16),
            pltpu.VMEM((2, KBLK * side, COL_GROUP * side), jnp.bfloat16),
            pltpu.VMEM((2, ROWB * side, COL_GROUP * side), jnp.float32),
            pltpu.VMEM((products, side, side), jnp.bfloat16),
            pltpu.SemaphoreType.DMA((2,)),
            pltpu.SemaphoreType.DMA((2,)),
            pltpu.SemaphoreType.DMA((1,)),
        ],
        compiler_params=pltpu.CompilerParams(vmem_limit_bytes=60 * 1024 * 1024),
        cost_estimate=pl.CostEstimate(
            flops=flops, bytes_accessed=tile_bytes + partial_bytes + slots * side * side * 2, transcendentals=0
        ),
    )(slot_of, left_index, left_next, columns, partial, outgoing)
    outgoing = outgoing.reshape(devices_all, capacity, side, side)
    received = lax.all_to_all(outgoing, ("row", "col"), split_axis=0, concat_axis=0, tiled=True)
    chunk = devices_all // COPY_STEPS
    block = pl.BlockSpec((chunk, capacity, side, side), lambda i: (i, 0, 0, 0))
    received = pl.pallas_call(
        pass_through,
        out_shape=jax.ShapeDtypeStruct(received.shape, received.dtype),
        grid=(COPY_STEPS,),
        in_specs=[block],
        out_specs=block,
        cost_estimate=pl.CostEstimate(flops=0, bytes_accessed=2 * received.size * 2, transcendentals=0),
    )(received)
    return received[None]


def solution(mesh):
    placed = (
        P("row", "col", None, None, None),
        P(),
        P("row", "col", None, None, None),
        P(),
        P(("row", "col"), None),
    )
    return jax.shard_map(
        body,
        mesh=mesh,
        in_specs=placed,
        out_specs=P(("row", "col"), None, None, None, None),
        check_vma=False,
    )
```

```python
import functools

import jax
import jax.numpy as jnp
from jax import lax
from jax.experimental import pallas as pl
from jax.experimental.pallas import tpu as pltpu
from jax.sharding import PartitionSpec as P

ROWB = 8
KBLK = 16
COLB = 16
COL_GROUP = 2
ROW_GROUP = 8
COPY_STEPS = 2


def from_behind(block, axis, distance):
    devices = range(lax.axis_size(axis))
    route = [((i - distance) % len(devices), i) for i in devices]
    return lax.ppermute(block, axis, route)


def fill(ref, count, value):
    def step(i, carry):
        ref[i] = value
        return carry

    lax.fori_loop(0, count, step, 0)


def invert_places(places, tile, index_ref, positions, stored):
    fill(index_ref, positions, -1)

    def step(n, carry):
        index_ref[places[tile[0], tile[1], n]] = n
        return carry

    lax.fori_loop(0, stored, step, 0)


def multiply_tiles(
    left_tile, right_tile, left_index, right_index, left_dense, right_column, emit, before=None,
    left_ready=None, right_ready=None, column_of=None,
):
    side = left_tile.shape[-1]
    zero_block = jnp.zeros((side, side), left_tile.dtype)
    if left_ready is not None:
        left_ready()

    def densify_left(r, carry):
        rows = pl.ds(pl.multiple_of(r * side, side), side)
        for k in range(KBLK):
            index = left_index[r * KBLK + k]
            block = left_tile[jnp.maximum(index, 0)]
            left_dense[rows, k * side:(k + 1) * side] = jnp.where(index >= 0, block, zero_block)
        return carry

    lax.fori_loop(0, ROWB, densify_left, 0)
    if right_ready is not None:
        right_ready()

    def place_column(cp, clear):
        if clear:
            return
        for k in range(KBLK):
            for cc in range(COL_GROUP):
                index = right_index[k * COLB + cp * COL_GROUP + cc]
                block = right_tile[jnp.maximum(index, 0)]
                right_column[k * side:(k + 1) * side, cc * side:(cc + 1) * side] = jnp.where(
                    index >= 0, block, zero_block
                )

    def column_pair(cp, carry):
        if before is not None:
            before(cp)
        if column_of is None:
            place_column(cp, False)
            column = right_column
        else:
            column = column_of(cp)

        def row_pair(rp, inner):
            rows = pl.ds(pl.multiple_of(rp * ROW_GROUP * side, ROW_GROUP * side), ROW_GROUP * side)
            result = jnp.dot(left_dense[rows, :], column[...], preferred_element_type=jnp.float32)
            emit(rp, cp, rows, result)
            return inner

        lax.fori_loop(0, ROWB // ROW_GROUP, row_pair, 0)
        if column_of is None:
            place_column(cp, True)
        return carry

    lax.fori_loop(0, COLB // COL_GROUP, column_pair, 0, unroll=column_of is not None)


def first_kernel(
    rows_grid, cols_grid, capacity,
    left_places, right_places, owners, left_tile, right_tile,
    partial, slot_of, left_index_next, right_index_next, outgoing,
    left_dense, right_column, left_index, right_index, counts, filled, zero_ref, zero_sems,
):
    side = left_tile.shape[-1]
    stored = left_tile.shape[0]
    row_here = lax.axis_index("row")
    col_here = lax.axis_index("col")
    row_next = lax.rem(row_here + 1, rows_grid)
    col_next = lax.rem(col_here + 1, cols_grid)
    invert_places(left_places, (row_here, col_here), left_index, ROWB * KBLK, stored)
    invert_places(right_places, (row_here, col_here), right_index, KBLK * COLB, stored)
    invert_places(left_places, (row_here, col_next), left_index_next, ROWB * KBLK, stored)
    invert_places(right_places, (row_next, col_here), right_index_next, KBLK * COLB, stored)
    fill(filled, filled.shape[0], 0)
    fill(counts, counts.shape[0], 0)

    def assign(m, carry):
        owner = owners[m]
        taken = counts[owner]
        slot = owner * capacity + taken
        slot_of[m] = slot
        filled[slot] = 1
        counts[owner] = taken + 1
        return carry

    lax.fori_loop(0, ROWB * COLB, assign, 0)
    zero_ref[...] = jnp.zeros(zero_ref.shape, zero_ref.dtype)

    def zero_slot(s, carry):
        @pl.when(filled[s] == 0)
        def _():
            pltpu.make_async_copy(zero_ref, outgoing.at[s], zero_sems.at[0]).start()

        return carry

    lax.fori_loop(0, outgoing.shape[0], zero_slot, 0)

    def emit(rp, cp, rows, result):
        partial[cp, rows, :] = result

    multiply_tiles(left_tile, right_tile, left_index, right_index, left_dense, right_column, emit)

    unfilled = outgoing.shape[0] - ROWB * COLB
    pltpu.make_async_copy(outgoing.at[pl.ds(0, unfilled)], outgoing.at[pl.ds(0, unfilled)], zero_sems.at[0]).wait()


def column_kernel(right_index, right_tile, columns, column_buf, sems):
    side = right_tile.shape[-1]
    pairs = COLB // COL_GROUP
    zero_block = jnp.zeros((side, side), right_tile.dtype)

    def send(cp, buffer):
        return pltpu.make_async_copy(column_buf.at[buffer], columns.at[cp], sems.at[buffer])

    def column_pair(cp, carry):
        buffer = lax.rem(cp, 2)

        @pl.when(cp >= 2)
        def _():
            send(cp - 2, buffer).wait()

        for k in range(KBLK):
            for cc in range(COL_GROUP):
                index = right_index[k * COLB + cp * COL_GROUP + cc]
                block = right_tile[jnp.maximum(index, 0)]
                column_buf[buffer, k * side:(k + 1) * side, cc * side:(cc + 1) * side] = jnp.where(
                    index >= 0, block, zero_block
                )
        send(cp, buffer).start()
        return carry

    lax.fori_loop(0, pairs, column_pair, 0)
    send(pairs - 2, 0).wait()
    send(pairs - 1, 1).wait()


def second_kernel(
    slot_of, left_index, left_tile, columns, partial, outgoing,
    out,
    left_dense, column_buf, partial_buf, staging, partial_sems, column_sems, out_sems,
):
    side = left_tile.shape[-1]
    pairs = COLB // COL_GROUP
    products = ROWB * COLB

    def partial_copy(cp, buffer):
        return pltpu.make_async_copy(partial.at[cp], partial_buf.at[buffer], partial_sems.at[buffer])

    def column_copy(cp, buffer):
        return pltpu.make_async_copy(columns.at[cp], column_buf.at[buffer], column_sems.at[buffer])

    partial_copy(0, 0).start()
    column_copy(0, 0).start()

    def send_pair(cp):
        for r in range(ROWB):
            for cc in range(COL_GROUP):
                m = r * COLB + cp * COL_GROUP + cc
                pltpu.make_async_copy(staging.at[m], out.at[slot_of[m]], out_sems.at[0]).start()

    def before(cp):
        buffer = lax.rem(cp, 2)

        @pl.when(cp + 1 < pairs)
        def _():
            partial_copy(cp + 1, 1 - buffer).start()
            column_copy(cp + 1, 1 - buffer).start()

        @pl.when(cp > 0)
        def _():
            send_pair(cp - 1)

        partial_copy(cp, buffer).wait()
        column_copy(cp, buffer).wait()

    def emit(rp, cp, rows, result):
        buffer = lax.rem(cp, 2)
        total = result + partial_buf[buffer, rows, :]
        for rr in range(ROW_GROUP):
            for cc in range(COL_GROUP):
                m = (rp * ROW_GROUP + rr) * COLB + cp * COL_GROUP + cc
                piece = total[rr * side:(rr + 1) * side, cc * side:(cc + 1) * side]
                staging[m] = piece.astype(staging.dtype)

    multiply_tiles(
        left_tile, None, left_index, None, left_dense, None, emit, before,
        column_of=lambda cp: column_buf.at[lax.rem(cp, 2)],
    )
    send_pair(pairs - 1)

    pltpu.make_async_copy(staging, out.at[pl.ds(0, products)], out_sems.at[0]).wait()


def pass_through(source, target):
    target[...] = source[...]


def body(left_values, left_places, right_values, right_places, owners):
    rows_grid = lax.axis_size("row")
    cols_grid = lax.axis_size("col")
    devices_all = rows_grid * cols_grid
    left_here = left_values[0, 0]
    right_here = right_values[0, 0]
    side = left_here.shape[-1]
    left_next = from_behind(left_here, "col", -1)
    right_next = from_behind(right_here, "row", -1)
    capacity = 2 * ROWB * COLB // devices_all
    slots = devices_all * capacity
    products = ROWB * COLB
    pairs = COLB // COL_GROUP
    smem = pl.BlockSpec(memory_space=pltpu.SMEM)
    vmem = pl.BlockSpec(memory_space=pltpu.VMEM)
    anywhere = pl.BlockSpec(memory_space=pl.ANY)
    work = [
        pltpu.VMEM((ROWB * side, KBLK * side), jnp.bfloat16),
        pltpu.VMEM((KBLK * side, COL_GROUP * side), jnp.bfloat16),
    ]
    flops = 2 * (ROWB * side) * (KBLK * side) * (COLB * side)
    tile_bytes = 2 * left_here.size * 2
    partial_bytes = ROWB * COLB * side * side * 4
    partial, slot_of, left_index, right_index, outgoing = pl.pallas_call(
        functools.partial(first_kernel, rows_grid, cols_grid, capacity),
        out_shape=(
            jax.ShapeDtypeStruct((pairs, ROWB * side, COL_GROUP * side), jnp.float32),
            jax.ShapeDtypeStruct((products,), jnp.int32),
            jax.ShapeDtypeStruct((ROWB * KBLK,), jnp.int32),
            jax.ShapeDtypeStruct((KBLK * COLB,), jnp.int32),
            jax.ShapeDtypeStruct((slots, side, side), jnp.bfloat16),
        ),
        in_specs=[smem, smem, smem, vmem, vmem],
        out_specs=(vmem, smem, smem, smem, anywhere),
        scratch_shapes=work + [
            pltpu.SMEM((ROWB * KBLK,), jnp.int32),
            pltpu.SMEM((KBLK * COLB,), jnp.int32),
            pltpu.SMEM((devices_all,), jnp.int32),
            pltpu.SMEM((slots,), jnp.int32),
            pltpu.VMEM((side, side), jnp.bfloat16),
            pltpu.SemaphoreType.DMA((1,)),
        ],
        compiler_params=pltpu.CompilerParams(vmem_limit_bytes=60 * 1024 * 1024),
        cost_estimate=pl.CostEstimate(flops=flops, bytes_accessed=tile_bytes + partial_bytes, transcendentals=0),
    )(left_places, right_places, owners[0], left_here, right_here)
    column_bytes = pairs * KBLK * side * COL_GROUP * side * 2
    columns = pl.pallas_call(
        column_kernel,
        out_shape=jax.ShapeDtypeStruct((pairs, KBLK * side, COL_GROUP * side), jnp.bfloat16),
        in_specs=[smem, vmem],
        out_specs=anywhere,
        scratch_shapes=[
            pltpu.VMEM((2, KBLK * side, COL_GROUP * side), jnp.bfloat16),
            pltpu.SemaphoreType.DMA((2,)),
        ],
        cost_estimate=pl.CostEstimate(flops=0, bytes_accessed=left_here.size * 2 + column_bytes, transcendentals=0),
    )(right_index, right_next)
    outgoing = pl.pallas_call(
        second_kernel,
        out_shape=jax.ShapeDtypeStruct((slots, side, side), jnp.bfloat16),
        in_specs=[smem, smem, vmem, anywhere, anywhere, anywhere],
        out_specs=anywhere,
        input_output_aliases={5: 0},
        scratch_shapes=[
            pltpu.VMEM((ROWB * side, KBLK * side), jnp.bfloat16),
            pltpu.VMEM((2, KBLK * side, COL_GROUP * side), jnp.bfloat16),
            pltpu.VMEM((2, ROWB * side, COL_GROUP * side), jnp.float32),
            pltpu.VMEM((products, side, side), jnp.bfloat16),
            pltpu.SemaphoreType.DMA((2,)),
            pltpu.SemaphoreType.DMA((2,)),
            pltpu.SemaphoreType.DMA((1,)),
        ],
        compiler_params=pltpu.CompilerParams(vmem_limit_bytes=60 * 1024 * 1024),
        cost_estimate=pl.CostEstimate(
            flops=flops, bytes_accessed=tile_bytes + partial_bytes + slots * side * side * 2, transcendentals=0
        ),
    )(slot_of, left_index, left_next, columns, partial, outgoing)
    outgoing = outgoing.reshape(devices_all, capacity, side, side)
    received = lax.all_to_all(outgoing, ("row", "col"), split_axis=0, concat_axis=0, tiled=True)
    chunk = devices_all // COPY_STEPS
    block = pl.BlockSpec((chunk, capacity, side, side), lambda i: (i, 0, 0, 0))
    received = pl.pallas_call(
        pass_through,
        out_shape=jax.ShapeDtypeStruct(received.shape, received.dtype),
        grid=(COPY_STEPS,),
        in_specs=[block],
        out_specs=block,
        cost_estimate=pl.CostEstimate(flops=0, bytes_accessed=2 * received.size * 2, transcendentals=0),
    )(received)
    return received[None]


def solution(mesh):
    placed = (
        P("row", "col", None, None, None),
        P(),
        P("row", "col", None, None, None),
        P(),
        P(("row", "col"), None),
    )
    return jax.shard_map(
        body,
        mesh=mesh,
        in_specs=placed,
        out_specs=P(("row", "col"), None, None, None, None),
        check_vma=False,
    )
```

```python
import functools

import jax
import jax.numpy as jnp
from jax import lax
from jax.experimental import pallas as pl
from jax.experimental.pallas import tpu as pltpu
from jax.sharding import PartitionSpec as P

ROWB = 8
KBLK = 16
COLB = 16
COL_GROUP = 4
ROW_GROUP = 8
COPY_STEPS = 2


def from_behind(block, axis, distance):
    devices = range(lax.axis_size(axis))
    route = [((i - distance) % len(devices), i) for i in devices]
    return lax.ppermute(block, axis, route)


def fill(ref, count, value):
    def step(i, carry):
        ref[i] = value
        return carry

    lax.fori_loop(0, count, step, 0)


def invert_places(places, tile, index_ref, positions, stored):
    fill(index_ref, positions, -1)

    def step(n, carry):
        index_ref[places[tile[0], tile[1], n]] = n
        return carry

    lax.fori_loop(0, stored, step, 0)


def multiply_tiles(
    left_tile, right_tile, left_index, right_index, left_dense, right_column, emit, before=None,
    left_ready=None, right_ready=None, column_of=None,
):
    side = left_tile.shape[-1]
    zero_block = jnp.zeros((side, side), left_tile.dtype)
    if left_ready is not None:
        left_ready()

    def densify_left(r, carry):
        rows = pl.ds(pl.multiple_of(r * side, side), side)
        for k in range(KBLK):
            index = left_index[r * KBLK + k]
            block = left_tile[jnp.maximum(index, 0)]
            left_dense[rows, k * side:(k + 1) * side] = jnp.where(index >= 0, block, zero_block)
        return carry

    lax.fori_loop(0, ROWB, densify_left, 0)
    if right_ready is not None:
        right_ready()

    def place_column(cp, clear):
        if clear:
            return
        for k in range(KBLK):
            for cc in range(COL_GROUP):
                index = right_index[k * COLB + cp * COL_GROUP + cc]
                block = right_tile[jnp.maximum(index, 0)]
                right_column[k * side:(k + 1) * side, cc * side:(cc + 1) * side] = jnp.where(
                    index >= 0, block, zero_block
                )

    def column_pair(cp, carry):
        if before is not None:
            before(cp)
        if column_of is None:
            place_column(cp, False)
            column = right_column
        else:
            column = column_of(cp)

        def row_pair(rp, inner):
            rows = pl.ds(pl.multiple_of(rp * ROW_GROUP * side, ROW_GROUP * side), ROW_GROUP * side)
            result = jnp.dot(left_dense[rows, :], column[...], preferred_element_type=jnp.float32)
            emit(rp, cp, rows, result)
            return inner

        lax.fori_loop(0, ROWB // ROW_GROUP, row_pair, 0)
        if column_of is None:
            place_column(cp, True)
        return carry

    lax.fori_loop(0, COLB // COL_GROUP, column_pair, 0)


def first_kernel(
    rows_grid, cols_grid, capacity,
    left_places, right_places, owners, left_tile, right_tile,
    partial, slot_of, left_index_next, right_index_next, outgoing,
    left_dense, right_column, left_index, right_index, counts, filled, zero_ref, zero_sems,
):
    side = left_tile.shape[-1]
    stored = left_tile.shape[0]
    row_here = lax.axis_index("row")
    col_here = lax.axis_index("col")
    row_next = lax.rem(row_here + 1, rows_grid)
    col_next = lax.rem(col_here + 1, cols_grid)
    invert_places(left_places, (row_here, col_here), left_index, ROWB * KBLK, stored)
    invert_places(right_places, (row_here, col_here), right_index, KBLK * COLB, stored)
    invert_places(left_places, (row_here, col_next), left_index_next, ROWB * KBLK, stored)
    invert_places(right_places, (row_next, col_here), right_index_next, KBLK * COLB, stored)
    fill(filled, filled.shape[0], 0)
    fill(counts, counts.shape[0], 0)

    def assign(m, carry):
        owner = owners[m]
        taken = counts[owner]
        slot = owner * capacity + taken
        slot_of[m] = slot
        filled[slot] = 1
        counts[owner] = taken + 1
        return carry

    lax.fori_loop(0, ROWB * COLB, assign, 0)
    zero_ref[...] = jnp.zeros(zero_ref.shape, zero_ref.dtype)

    def zero_slot(s, carry):
        @pl.when(filled[s] == 0)
        def _():
            pltpu.make_async_copy(zero_ref, outgoing.at[s], zero_sems.at[0]).start()

        return carry

    lax.fori_loop(0, outgoing.shape[0], zero_slot, 0)

    def emit(rp, cp, rows, result):
        partial[cp, rows, :] = result

    multiply_tiles(left_tile, right_tile, left_index, right_index, left_dense, right_column, emit)

    unfilled = outgoing.shape[0] - ROWB * COLB
    pltpu.make_async_copy(outgoing.at[pl.ds(0, unfilled)], outgoing.at[pl.ds(0, unfilled)], zero_sems.at[0]).wait()


def column_kernel(right_index, right_tile, columns, column_buf, sems):
    side = right_tile.shape[-1]
    pairs = COLB // COL_GROUP
    zero_block = jnp.zeros((side, side), right_tile.dtype)

    def send(cp, buffer):
        return pltpu.make_async_copy(column_buf.at[buffer], columns.at[cp], sems.at[buffer])

    def column_pair(cp, carry):
        buffer = lax.rem(cp, 2)

        @pl.when(cp >= 2)
        def _():
            send(cp - 2, buffer).wait()

        for k in range(KBLK):
            for cc in range(COL_GROUP):
                index = right_index[k * COLB + cp * COL_GROUP + cc]
                block = right_tile[jnp.maximum(index, 0)]
                column_buf[buffer, k * side:(k + 1) * side, cc * side:(cc + 1) * side] = jnp.where(
                    index >= 0, block, zero_block
                )
        send(cp, buffer).start()
        return carry

    lax.fori_loop(0, pairs, column_pair, 0)
    send(pairs - 2, 0).wait()
    send(pairs - 1, 1).wait()


def second_kernel(
    slot_of, left_index, left_tile, columns, partial, outgoing,
    out,
    left_dense, column_buf, partial_buf, staging, partial_sems, column_sems, out_sems,
):
    side = left_tile.shape[-1]
    pairs = COLB // COL_GROUP
    products = ROWB * COLB

    def partial_copy(cp, buffer):
        return pltpu.make_async_copy(partial.at[cp], partial_buf.at[buffer], partial_sems.at[buffer])

    def column_copy(cp, buffer):
        return pltpu.make_async_copy(columns.at[cp], column_buf.at[buffer], column_sems.at[buffer])

    partial_copy(0, 0).start()
    column_copy(0, 0).start()

    def send_pair(cp):
        for r in range(ROWB):
            for cc in range(COL_GROUP):
                m = r * COLB + cp * COL_GROUP + cc
                pltpu.make_async_copy(staging.at[m], out.at[slot_of[m]], out_sems.at[0]).start()

    def before(cp):
        buffer = lax.rem(cp, 2)

        @pl.when(cp + 1 < pairs)
        def _():
            partial_copy(cp + 1, 1 - buffer).start()
            column_copy(cp + 1, 1 - buffer).start()

        @pl.when(cp > 0)
        def _():
            send_pair(cp - 1)

        partial_copy(cp, buffer).wait()
        column_copy(cp, buffer).wait()

    def emit(rp, cp, rows, result):
        buffer = lax.rem(cp, 2)
        total = result + partial_buf[buffer, rows, :]
        for rr in range(ROW_GROUP):
            for cc in range(COL_GROUP):
                m = (rp * ROW_GROUP + rr) * COLB + cp * COL_GROUP + cc
                piece = total[rr * side:(rr + 1) * side, cc * side:(cc + 1) * side]
                staging[m] = piece.astype(staging.dtype)

    multiply_tiles(
        left_tile, None, left_index, None, left_dense, None, emit, before,
        column_of=lambda cp: column_buf.at[lax.rem(cp, 2)],
    )
    send_pair(pairs - 1)

    pltpu.make_async_copy(staging, out.at[pl.ds(0, products)], out_sems.at[0]).wait()


def pass_through(source, target):
    target[...] = source[...]


def body(left_values, left_places, right_values, right_places, owners):
    rows_grid = lax.axis_size("row")
    cols_grid = lax.axis_size("col")
    devices_all = rows_grid * cols_grid
    left_here = left_values[0, 0]
    right_here = right_values[0, 0]
    side = left_here.shape[-1]
    left_next = from_behind(left_here, "col", -1)
    right_next = from_behind(right_here, "row", -1)
    capacity = 2 * ROWB * COLB // devices_all
    slots = devices_all * capacity
    products = ROWB * COLB
    pairs = COLB // COL_GROUP
    smem = pl.BlockSpec(memory_space=pltpu.SMEM)
    vmem = pl.BlockSpec(memory_space=pltpu.VMEM)
    anywhere = pl.BlockSpec(memory_space=pl.ANY)
    work = [
        pltpu.VMEM((ROWB * side, KBLK * side), jnp.bfloat16),
        pltpu.VMEM((KBLK * side, COL_GROUP * side), jnp.bfloat16),
    ]
    flops = 2 * (ROWB * side) * (KBLK * side) * (COLB * side)
    tile_bytes = 2 * left_here.size * 2
    partial_bytes = ROWB * COLB * side * side * 4
    partial, slot_of, left_index, right_index, outgoing = pl.pallas_call(
        functools.partial(first_kernel, rows_grid, cols_grid, capacity),
        out_shape=(
            jax.ShapeDtypeStruct((pairs, ROWB * side, COL_GROUP * side), jnp.float32),
            jax.ShapeDtypeStruct((products,), jnp.int32),
            jax.ShapeDtypeStruct((ROWB * KBLK,), jnp.int32),
            jax.ShapeDtypeStruct((KBLK * COLB,), jnp.int32),
            jax.ShapeDtypeStruct((slots, side, side), jnp.bfloat16),
        ),
        in_specs=[smem, smem, smem, vmem, vmem],
        out_specs=(vmem, smem, smem, smem, anywhere),
        scratch_shapes=work + [
            pltpu.SMEM((ROWB * KBLK,), jnp.int32),
            pltpu.SMEM((KBLK * COLB,), jnp.int32),
            pltpu.SMEM((devices_all,), jnp.int32),
            pltpu.SMEM((slots,), jnp.int32),
            pltpu.VMEM((side, side), jnp.bfloat16),
            pltpu.SemaphoreType.DMA((1,)),
        ],
        compiler_params=pltpu.CompilerParams(vmem_limit_bytes=60 * 1024 * 1024),
        cost_estimate=pl.CostEstimate(flops=flops, bytes_accessed=tile_bytes + partial_bytes, transcendentals=0),
    )(left_places, right_places, owners[0], left_here, right_here)
    column_bytes = pairs * KBLK * side * COL_GROUP * side * 2
    columns = pl.pallas_call(
        column_kernel,
        out_shape=jax.ShapeDtypeStruct((pairs, KBLK * side, COL_GROUP * side), jnp.bfloat16),
        in_specs=[smem, vmem],
        out_specs=anywhere,
        scratch_shapes=[
            pltpu.VMEM((2, KBLK * side, COL_GROUP * side), jnp.bfloat16),
            pltpu.SemaphoreType.DMA((2,)),
        ],
        cost_estimate=pl.CostEstimate(flops=0, bytes_accessed=left_here.size * 2 + column_bytes, transcendentals=0),
    )(right_index, right_next)
    outgoing = pl.pallas_call(
        second_kernel,
        out_shape=jax.ShapeDtypeStruct((slots, side, side), jnp.bfloat16),
        in_specs=[smem, smem, vmem, anywhere, anywhere, anywhere],
        out_specs=anywhere,
        input_output_aliases={5: 0},
        scratch_shapes=[
            pltpu.VMEM((ROWB * side, KBLK * side), jnp.bfloat16),
            pltpu.VMEM((2, KBLK * side, COL_GROUP * side), jnp.bfloat16),
            pltpu.VMEM((2, ROWB * side, COL_GROUP * side), jnp.float32),
            pltpu.VMEM((products, side, side), jnp.bfloat16),
            pltpu.SemaphoreType.DMA((2,)),
            pltpu.SemaphoreType.DMA((2,)),
            pltpu.SemaphoreType.DMA((1,)),
        ],
        compiler_params=pltpu.CompilerParams(vmem_limit_bytes=60 * 1024 * 1024),
        cost_estimate=pl.CostEstimate(
            flops=flops, bytes_accessed=tile_bytes + partial_bytes + slots * side * side * 2, transcendentals=0
        ),
    )(slot_of, left_index, left_next, columns, partial, outgoing)
    outgoing = outgoing.reshape(devices_all, capacity, side, side)
    received = lax.all_to_all(outgoing, ("row", "col"), split_axis=0, concat_axis=0, tiled=True)
    chunk = devices_all // COPY_STEPS
    block = pl.BlockSpec((chunk, capacity, side, side), lambda i: (i, 0, 0, 0))
    received = pl.pallas_call(
        pass_through,
        out_shape=jax.ShapeDtypeStruct(received.shape, received.dtype),
        grid=(COPY_STEPS,),
        in_specs=[block],
        out_specs=block,
        cost_estimate=pl.CostEstimate(flops=0, bytes_accessed=2 * received.size * 2, transcendentals=0),
    )(received)
    return received[None]


def solution(mesh):
    placed = (
        P("row", "col", None, None, None),
        P(),
        P("row", "col", None, None, None),
        P(),
        P(("row", "col"), None),
    )
    return jax.shard_map(
        body,
        mesh=mesh,
        in_specs=placed,
        out_specs=P(("row", "col"), None, None, None, None),
        check_vma=False,
    )
```

```python
import functools

import jax
import jax.numpy as jnp
from jax import lax
from jax.experimental import pallas as pl
from jax.experimental.pallas import tpu as pltpu
from jax.sharding import PartitionSpec as P

ROWB = 8
KBLK = 16
COLB = 16
COL_GROUP = 8
ROW_GROUP = 8
COPY_STEPS = 2


def from_behind(block, axis, distance):
    devices = range(lax.axis_size(axis))
    route = [((i - distance) % len(devices), i) for i in devices]
    return lax.ppermute(block, axis, route)


def fill(ref, count, value):
    def step(i, carry):
        ref[i] = value
        return carry

    lax.fori_loop(0, count, step, 0)


def invert_places(places, tile, index_ref, positions, stored):
    fill(index_ref, positions, -1)

    def step(n, carry):
        index_ref[places[tile[0], tile[1], n]] = n
        return carry

    lax.fori_loop(0, stored, step, 0)


def multiply_tiles(
    left_tile, right_tile, left_index, right_index, left_dense, right_column, emit, before=None,
    left_ready=None, right_ready=None, column_of=None,
):
    side = left_tile.shape[-1]
    zero_block = jnp.zeros((side, side), left_tile.dtype)
    if left_ready is not None:
        left_ready()

    def densify_left(r, carry):
        rows = pl.ds(pl.multiple_of(r * side, side), side)
        for k in range(KBLK):
            index = left_index[r * KBLK + k]
            block = left_tile[jnp.maximum(index, 0)]
            left_dense[rows, k * side:(k + 1) * side] = jnp.where(index >= 0, block, zero_block)
        return carry

    lax.fori_loop(0, ROWB, densify_left, 0)
    if right_ready is not None:
        right_ready()

    def place_column(cp, clear):
        if clear:
            return
        for k in range(KBLK):
            for cc in range(COL_GROUP):
                index = right_index[k * COLB + cp * COL_GROUP + cc]
                block = right_tile[jnp.maximum(index, 0)]
                right_column[k * side:(k + 1) * side, cc * side:(cc + 1) * side] = jnp.where(
                    index >= 0, block, zero_block
                )

    def column_pair(cp, carry):
        if before is not None:
            before(cp)
        if column_of is None:
            place_column(cp, False)
            column = right_column
        else:
            column = column_of(cp)

        def row_pair(rp, inner):
            rows = pl.ds(pl.multiple_of(rp * ROW_GROUP * side, ROW_GROUP * side), ROW_GROUP * side)
            result = jnp.dot(left_dense[rows, :], column[...], preferred_element_type=jnp.float32)
            emit(rp, cp, rows, result)
            return inner

        lax.fori_loop(0, ROWB // ROW_GROUP, row_pair, 0)
        if column_of is None:
            place_column(cp, True)
        return carry

    lax.fori_loop(0, COLB // COL_GROUP, column_pair, 0)


def first_kernel(
    rows_grid, cols_grid, capacity,
    left_places, right_places, owners, left_tile, right_tile,
    partial, slot_of, left_index_next, right_index_next, outgoing,
    left_dense, right_column, left_index, right_index, counts, filled, zero_ref, zero_sems,
):
    side = left_tile.shape[-1]
    stored = left_tile.shape[0]
    row_here = lax.axis_index("row")
    col_here = lax.axis_index("col")
    row_next = lax.rem(row_here + 1, rows_grid)
    col_next = lax.rem(col_here + 1, cols_grid)
    invert_places(left_places, (row_here, col_here), left_index, ROWB * KBLK, stored)
    invert_places(right_places, (row_here, col_here), right_index, KBLK * COLB, stored)
    invert_places(left_places, (row_here, col_next), left_index_next, ROWB * KBLK, stored)
    invert_places(right_places, (row_next, col_here), right_index_next, KBLK * COLB, stored)
    fill(filled, filled.shape[0], 0)
    fill(counts, counts.shape[0], 0)

    def assign(m, carry):
        owner = owners[m]
        taken = counts[owner]
        slot = owner * capacity + taken
        slot_of[m] = slot
        filled[slot] = 1
        counts[owner] = taken + 1
        return carry

    lax.fori_loop(0, ROWB * COLB, assign, 0)
    zero_ref[...] = jnp.zeros(zero_ref.shape, zero_ref.dtype)

    def zero_slot(s, carry):
        @pl.when(filled[s] == 0)
        def _():
            pltpu.make_async_copy(zero_ref, outgoing.at[s], zero_sems.at[0]).start()

        return carry

    lax.fori_loop(0, outgoing.shape[0], zero_slot, 0)

    def emit(rp, cp, rows, result):
        partial[cp, rows, :] = result

    multiply_tiles(left_tile, right_tile, left_index, right_index, left_dense, right_column, emit)

    unfilled = outgoing.shape[0] - ROWB * COLB
    pltpu.make_async_copy(outgoing.at[pl.ds(0, unfilled)], outgoing.at[pl.ds(0, unfilled)], zero_sems.at[0]).wait()


def column_kernel(right_index, right_tile, columns, column_buf, sems):
    side = right_tile.shape[-1]
    pairs = COLB // COL_GROUP
    zero_block = jnp.zeros((side, side), right_tile.dtype)

    def send(cp, buffer):
        return pltpu.make_async_copy(column_buf.at[buffer], columns.at[cp], sems.at[buffer])

    def column_pair(cp, carry):
        buffer = lax.rem(cp, 2)

        @pl.when(cp >= 2)
        def _():
            send(cp - 2, buffer).wait()

        for k in range(KBLK):
            for cc in range(COL_GROUP):
                index = right_index[k * COLB + cp * COL_GROUP + cc]
                block = right_tile[jnp.maximum(index, 0)]
                column_buf[buffer, k * side:(k + 1) * side, cc * side:(cc + 1) * side] = jnp.where(
                    index >= 0, block, zero_block
                )
        send(cp, buffer).start()
        return carry

    lax.fori_loop(0, pairs, column_pair, 0)
    send(pairs - 2, 0).wait()
    send(pairs - 1, 1).wait()


def second_kernel(
    slot_of, left_index, left_tile, columns, partial, outgoing,
    out,
    left_dense, column_buf, partial_buf, staging, partial_sems, column_sems, out_sems,
):
    side = left_tile.shape[-1]
    pairs = COLB // COL_GROUP
    products = ROWB * COLB

    def partial_copy(cp, buffer):
        return pltpu.make_async_copy(partial.at[cp], partial_buf.at[buffer], partial_sems.at[buffer])

    def column_copy(cp, buffer):
        return pltpu.make_async_copy(columns.at[cp], column_buf.at[buffer], column_sems.at[buffer])

    partial_copy(0, 0).start()
    column_copy(0, 0).start()

    def send_pair(cp):
        for r in range(ROWB):
            for cc in range(COL_GROUP):
                m = r * COLB + cp * COL_GROUP + cc
                pltpu.make_async_copy(staging.at[m], out.at[slot_of[m]], out_sems.at[0]).start()

    def before(cp):
        buffer = lax.rem(cp, 2)

        @pl.when(cp + 1 < pairs)
        def _():
            partial_copy(cp + 1, 1 - buffer).start()
            column_copy(cp + 1, 1 - buffer).start()

        @pl.when(cp > 0)
        def _():
            send_pair(cp - 1)

        partial_copy(cp, buffer).wait()
        column_copy(cp, buffer).wait()

    def emit(rp, cp, rows, result):
        buffer = lax.rem(cp, 2)
        total = result + partial_buf[buffer, rows, :]
        for rr in range(ROW_GROUP):
            for cc in range(COL_GROUP):
                m = (rp * ROW_GROUP + rr) * COLB + cp * COL_GROUP + cc
                piece = total[rr * side:(rr + 1) * side, cc * side:(cc + 1) * side]
                staging[m] = piece.astype(staging.dtype)

    multiply_tiles(
        left_tile, None, left_index, None, left_dense, None, emit, before,
        column_of=lambda cp: column_buf.at[lax.rem(cp, 2)],
    )
    send_pair(pairs - 1)

    pltpu.make_async_copy(staging, out.at[pl.ds(0, products)], out_sems.at[0]).wait()


def pass_through(source, target):
    target[...] = source[...]


def body(left_values, left_places, right_values, right_places, owners):
    rows_grid = lax.axis_size("row")
    cols_grid = lax.axis_size("col")
    devices_all = rows_grid * cols_grid
    left_here = left_values[0, 0]
    right_here = right_values[0, 0]
    side = left_here.shape[-1]
    left_next = from_behind(left_here, "col", -1)
    right_next = from_behind(right_here, "row", -1)
    capacity = 2 * ROWB * COLB // devices_all
    slots = devices_all * capacity
    products = ROWB * COLB
    pairs = COLB // COL_GROUP
    smem = pl.BlockSpec(memory_space=pltpu.SMEM)
    vmem = pl.BlockSpec(memory_space=pltpu.VMEM)
    anywhere = pl.BlockSpec(memory_space=pl.ANY)
    work = [
        pltpu.VMEM((ROWB * side, KBLK * side), jnp.bfloat16),
        pltpu.VMEM((KBLK * side, COL_GROUP * side), jnp.bfloat16),
    ]
    flops = 2 * (ROWB * side) * (KBLK * side) * (COLB * side)
    tile_bytes = 2 * left_here.size * 2
    partial_bytes = ROWB * COLB * side * side * 4
    partial, slot_of, left_index, right_index, outgoing = pl.pallas_call(
        functools.partial(first_kernel, rows_grid, cols_grid, capacity),
        out_shape=(
            jax.ShapeDtypeStruct((pairs, ROWB * side, COL_GROUP * side), jnp.float32),
            jax.ShapeDtypeStruct((products,), jnp.int32),
            jax.ShapeDtypeStruct((ROWB * KBLK,), jnp.int32),
            jax.ShapeDtypeStruct((KBLK * COLB,), jnp.int32),
            jax.ShapeDtypeStruct((slots, side, side), jnp.bfloat16),
        ),
        in_specs=[smem, smem, smem, vmem, vmem],
        out_specs=(vmem, smem, smem, smem, anywhere),
        scratch_shapes=work + [
            pltpu.SMEM((ROWB * KBLK,), jnp.int32),
            pltpu.SMEM((KBLK * COLB,), jnp.int32),
            pltpu.SMEM((devices_all,), jnp.int32),
            pltpu.SMEM((slots,), jnp.int32),
            pltpu.VMEM((side, side), jnp.bfloat16),
            pltpu.SemaphoreType.DMA((1,)),
        ],
        compiler_params=pltpu.CompilerParams(vmem_limit_bytes=60 * 1024 * 1024),
        cost_estimate=pl.CostEstimate(flops=flops, bytes_accessed=tile_bytes + partial_bytes, transcendentals=0),
    )(left_places, right_places, owners[0], left_here, right_here)
    column_bytes = pairs * KBLK * side * COL_GROUP * side * 2
    columns = pl.pallas_call(
        column_kernel,
        out_shape=jax.ShapeDtypeStruct((pairs, KBLK * side, COL_GROUP * side), jnp.bfloat16),
        in_specs=[smem, vmem],
        out_specs=anywhere,
        scratch_shapes=[
            pltpu.VMEM((2, KBLK * side, COL_GROUP * side), jnp.bfloat16),
            pltpu.SemaphoreType.DMA((2,)),
        ],
        cost_estimate=pl.CostEstimate(flops=0, bytes_accessed=left_here.size * 2 + column_bytes, transcendentals=0),
    )(right_index, right_next)
    outgoing = pl.pallas_call(
        second_kernel,
        out_shape=jax.ShapeDtypeStruct((slots, side, side), jnp.bfloat16),
        in_specs=[smem, smem, vmem, anywhere, anywhere, anywhere],
        out_specs=anywhere,
        input_output_aliases={5: 0},
        scratch_shapes=[
            pltpu.VMEM((ROWB * side, KBLK * side), jnp.bfloat16),
            pltpu.VMEM((2, KBLK * side, COL_GROUP * side), jnp.bfloat16),
            pltpu.VMEM((2, ROWB * side, COL_GROUP * side), jnp.float32),
            pltpu.VMEM((products, side, side), jnp.bfloat16),
            pltpu.SemaphoreType.DMA((2,)),
            pltpu.SemaphoreType.DMA((2,)),
            pltpu.SemaphoreType.DMA((1,)),
        ],
        compiler_params=pltpu.CompilerParams(vmem_limit_bytes=60 * 1024 * 1024),
        cost_estimate=pl.CostEstimate(
            flops=flops, bytes_accessed=tile_bytes + partial_bytes + slots * side * side * 2, transcendentals=0
        ),
    )(slot_of, left_index, left_next, columns, partial, outgoing)
    outgoing = outgoing.reshape(devices_all, capacity, side, side)
    received = lax.all_to_all(outgoing, ("row", "col"), split_axis=0, concat_axis=0, tiled=True)
    chunk = devices_all // COPY_STEPS
    block = pl.BlockSpec((chunk, capacity, side, side), lambda i: (i, 0, 0, 0))
    received = pl.pallas_call(
        pass_through,
        out_shape=jax.ShapeDtypeStruct(received.shape, received.dtype),
        grid=(COPY_STEPS,),
        in_specs=[block],
        out_specs=block,
        cost_estimate=pl.CostEstimate(flops=0, bytes_accessed=2 * received.size * 2, transcendentals=0),
    )(received)
    return received[None]


def solution(mesh):
    placed = (
        P("row", "col", None, None, None),
        P(),
        P("row", "col", None, None, None),
        P(),
        P(("row", "col"), None),
    )
    return jax.shard_map(
        body,
        mesh=mesh,
        in_specs=placed,
        out_specs=P(("row", "col"), None, None, None, None),
        check_vma=False,
    )
```

```python
import functools

import jax
import jax.numpy as jnp
from jax import lax
from jax.experimental import pallas as pl
from jax.experimental.pallas import tpu as pltpu
from jax.sharding import PartitionSpec as P

ROWB = 8
KBLK = 16
COLB = 16
COL_GROUP = 4
ROW_GROUP = 4
COPY_STEPS = 2


def from_behind(block, axis, distance):
    devices = range(lax.axis_size(axis))
    route = [((i - distance) % len(devices), i) for i in devices]
    return lax.ppermute(block, axis, route)


def fill(ref, count, value):
    def step(i, carry):
        ref[i] = value
        return carry

    lax.fori_loop(0, count, step, 0)


def invert_places(places, tile, index_ref, positions, stored):
    fill(index_ref, positions, -1)

    def step(n, carry):
        index_ref[places[tile[0], tile[1], n]] = n
        return carry

    lax.fori_loop(0, stored, step, 0)


def multiply_tiles(
    left_tile, right_tile, left_index, right_index, left_dense, right_column, emit, before=None,
    left_ready=None, right_ready=None, column_of=None,
):
    side = left_tile.shape[-1]
    zero_block = jnp.zeros((side, side), left_tile.dtype)
    if left_ready is not None:
        left_ready()

    def densify_left(r, carry):
        rows = pl.ds(pl.multiple_of(r * side, side), side)
        for k in range(KBLK):
            index = left_index[r * KBLK + k]
            block = left_tile[jnp.maximum(index, 0)]
            left_dense[rows, k * side:(k + 1) * side] = jnp.where(index >= 0, block, zero_block)
        return carry

    lax.fori_loop(0, ROWB, densify_left, 0)
    if right_ready is not None:
        right_ready()

    def place_column(cp, clear):
        if clear:
            return
        for k in range(KBLK):
            for cc in range(COL_GROUP):
                index = right_index[k * COLB + cp * COL_GROUP + cc]
                block = right_tile[jnp.maximum(index, 0)]
                right_column[k * side:(k + 1) * side, cc * side:(cc + 1) * side] = jnp.where(
                    index >= 0, block, zero_block
                )

    def column_pair(cp, carry):
        if before is not None:
            before(cp)
        if column_of is None:
            place_column(cp, False)
            column = right_column
        else:
            column = column_of(cp)

        def row_pair(rp, inner):
            rows = pl.ds(pl.multiple_of(rp * ROW_GROUP * side, ROW_GROUP * side), ROW_GROUP * side)
            result = jnp.dot(left_dense[rows, :], column[...], preferred_element_type=jnp.float32)
            emit(rp, cp, rows, result)
            return inner

        lax.fori_loop(0, ROWB // ROW_GROUP, row_pair, 0)
        if column_of is None:
            place_column(cp, True)
        return carry

    lax.fori_loop(0, COLB // COL_GROUP, column_pair, 0)


def first_kernel(
    rows_grid, cols_grid, capacity,
    left_places, right_places, owners, left_tile, right_tile,
    partial, slot_of, left_index_next, right_index_next, outgoing,
    left_dense, right_column, left_index, right_index, counts, filled, zero_ref, zero_sems,
):
    side = left_tile.shape[-1]
    stored = left_tile.shape[0]
    row_here = lax.axis_index("row")
    col_here = lax.axis_index("col")
    row_next = lax.rem(row_here + 1, rows_grid)
    col_next = lax.rem(col_here + 1, cols_grid)
    invert_places(left_places, (row_here, col_here), left_index, ROWB * KBLK, stored)
    invert_places(right_places, (row_here, col_here), right_index, KBLK * COLB, stored)
    invert_places(left_places, (row_here, col_next), left_index_next, ROWB * KBLK, stored)
    invert_places(right_places, (row_next, col_here), right_index_next, KBLK * COLB, stored)
    fill(filled, filled.shape[0], 0)
    fill(counts, counts.shape[0], 0)

    def assign(m, carry):
        owner = owners[m]
        taken = counts[owner]
        slot = owner * capacity + taken
        slot_of[m] = slot
        filled[slot] = 1
        counts[owner] = taken + 1
        return carry

    lax.fori_loop(0, ROWB * COLB, assign, 0)
    zero_ref[...] = jnp.zeros(zero_ref.shape, zero_ref.dtype)

    def zero_slot(s, carry):
        @pl.when(filled[s] == 0)
        def _():
            pltpu.make_async_copy(zero_ref, outgoing.at[s], zero_sems.at[0]).start()

        return carry

    lax.fori_loop(0, outgoing.shape[0], zero_slot, 0)

    def emit(rp, cp, rows, result):
        partial[cp, rows, :] = result

    multiply_tiles(left_tile, right_tile, left_index, right_index, left_dense, right_column, emit)

    unfilled = outgoing.shape[0] - ROWB * COLB
    pltpu.make_async_copy(outgoing.at[pl.ds(0, unfilled)], outgoing.at[pl.ds(0, unfilled)], zero_sems.at[0]).wait()


def column_kernel(right_index, right_tile, columns, column_buf, sems):
    side = right_tile.shape[-1]
    pairs = COLB // COL_GROUP
    zero_block = jnp.zeros((side, side), right_tile.dtype)

    def send(cp, buffer):
        return pltpu.make_async_copy(column_buf.at[buffer], columns.at[cp], sems.at[buffer])

    def column_pair(cp, carry):
        buffer = lax.rem(cp, 2)

        @pl.when(cp >= 2)
        def _():
            send(cp - 2, buffer).wait()

        for k in range(KBLK):
            for cc in range(COL_GROUP):
                index = right_index[k * COLB + cp * COL_GROUP + cc]
                block = right_tile[jnp.maximum(index, 0)]
                column_buf[buffer, k * side:(k + 1) * side, cc * side:(cc + 1) * side] = jnp.where(
                    index >= 0, block, zero_block
                )
        send(cp, buffer).start()
        return carry

    lax.fori_loop(0, pairs, column_pair, 0)
    send(pairs - 2, 0).wait()
    send(pairs - 1, 1).wait()


def second_kernel(
    slot_of, left_index, left_tile, columns, partial, outgoing,
    out,
    left_dense, column_buf, partial_buf, staging, partial_sems, column_sems, out_sems,
):
    side = left_tile.shape[-1]
    pairs = COLB // COL_GROUP
    products = ROWB * COLB

    def partial_copy(cp, buffer):
        return pltpu.make_async_copy(partial.at[cp], partial_buf.at[buffer], partial_sems.at[buffer])

    def column_copy(cp, buffer):
        return pltpu.make_async_copy(columns.at[cp], column_buf.at[buffer], column_sems.at[buffer])

    partial_copy(0, 0).start()
    column_copy(0, 0).start()

    def send_pair(cp):
        for r in range(ROWB):
            for cc in range(COL_GROUP):
                m = r * COLB + cp * COL_GROUP + cc
                pltpu.make_async_copy(staging.at[m], out.at[slot_of[m]], out_sems.at[0]).start()

    def before(cp):
        buffer = lax.rem(cp, 2)

        @pl.when(cp + 1 < pairs)
        def _():
            partial_copy(cp + 1, 1 - buffer).start()
            column_copy(cp + 1, 1 - buffer).start()

        @pl.when(cp > 0)
        def _():
            send_pair(cp - 1)

        partial_copy(cp, buffer).wait()
        column_copy(cp, buffer).wait()

    def emit(rp, cp, rows, result):
        buffer = lax.rem(cp, 2)
        total = result + partial_buf[buffer, rows, :]
        for rr in range(ROW_GROUP):
            for cc in range(COL_GROUP):
                m = (rp * ROW_GROUP + rr) * COLB + cp * COL_GROUP + cc
                piece = total[rr * side:(rr + 1) * side, cc * side:(cc + 1) * side]
                staging[m] = piece.astype(staging.dtype)

    multiply_tiles(
        left_tile, None, left_index, None, left_dense, None, emit, before,
        column_of=lambda cp: column_buf.at[lax.rem(cp, 2)],
    )
    send_pair(pairs - 1)

    pltpu.make_async_copy(staging, out.at[pl.ds(0, products)], out_sems.at[0]).wait()


def pass_through(source, target):
    target[...] = source[...]


def body(left_values, left_places, right_values, right_places, owners):
    rows_grid = lax.axis_size("row")
    cols_grid = lax.axis_size("col")
    devices_all = rows_grid * cols_grid
    left_here = left_values[0, 0]
    right_here = right_values[0, 0]
    side = left_here.shape[-1]
    left_next = from_behind(left_here, "col", -1)
    right_next = from_behind(right_here, "row", -1)
    capacity = 2 * ROWB * COLB // devices_all
    slots = devices_all * capacity
    products = ROWB * COLB
    pairs = COLB // COL_GROUP
    smem = pl.BlockSpec(memory_space=pltpu.SMEM)
    vmem = pl.BlockSpec(memory_space=pltpu.VMEM)
    anywhere = pl.BlockSpec(memory_space=pl.ANY)
    work = [
        pltpu.VMEM((ROWB * side, KBLK * side), jnp.bfloat16),
        pltpu.VMEM((KBLK * side, COL_GROUP * side), jnp.bfloat16),
    ]
    flops = 2 * (ROWB * side) * (KBLK * side) * (COLB * side)
    tile_bytes = 2 * left_here.size * 2
    partial_bytes = ROWB * COLB * side * side * 4
    partial, slot_of, left_index, right_index, outgoing = pl.pallas_call(
        functools.partial(first_kernel, rows_grid, cols_grid, capacity),
        out_shape=(
            jax.ShapeDtypeStruct((pairs, ROWB * side, COL_GROUP * side), jnp.float32),
            jax.ShapeDtypeStruct((products,), jnp.int32),
            jax.ShapeDtypeStruct((ROWB * KBLK,), jnp.int32),
            jax.ShapeDtypeStruct((KBLK * COLB,), jnp.int32),
            jax.ShapeDtypeStruct((slots, side, side), jnp.bfloat16),
        ),
        in_specs=[smem, smem, smem, vmem, vmem],
        out_specs=(vmem, smem, smem, smem, anywhere),
        scratch_shapes=work + [
            pltpu.SMEM((ROWB * KBLK,), jnp.int32),
            pltpu.SMEM((KBLK * COLB,), jnp.int32),
            pltpu.SMEM((devices_all,), jnp.int32),
            pltpu.SMEM((slots,), jnp.int32),
            pltpu.VMEM((side, side), jnp.bfloat16),
            pltpu.SemaphoreType.DMA((1,)),
        ],
        compiler_params=pltpu.CompilerParams(vmem_limit_bytes=60 * 1024 * 1024),
        cost_estimate=pl.CostEstimate(flops=flops, bytes_accessed=tile_bytes + partial_bytes, transcendentals=0),
    )(left_places, right_places, owners[0], left_here, right_here)
    column_bytes = pairs * KBLK * side * COL_GROUP * side * 2
    columns = pl.pallas_call(
        column_kernel,
        out_shape=jax.ShapeDtypeStruct((pairs, KBLK * side, COL_GROUP * side), jnp.bfloat16),
        in_specs=[smem, vmem],
        out_specs=anywhere,
        scratch_shapes=[
            pltpu.VMEM((2, KBLK * side, COL_GROUP * side), jnp.bfloat16),
            pltpu.SemaphoreType.DMA((2,)),
        ],
        cost_estimate=pl.CostEstimate(flops=0, bytes_accessed=left_here.size * 2 + column_bytes, transcendentals=0),
    )(right_index, right_next)
    outgoing = pl.pallas_call(
        second_kernel,
        out_shape=jax.ShapeDtypeStruct((slots, side, side), jnp.bfloat16),
        in_specs=[smem, smem, vmem, anywhere, anywhere, anywhere],
        out_specs=anywhere,
        input_output_aliases={5: 0},
        scratch_shapes=[
            pltpu.VMEM((ROWB * side, KBLK * side), jnp.bfloat16),
            pltpu.VMEM((2, KBLK * side, COL_GROUP * side), jnp.bfloat16),
            pltpu.VMEM((2, ROWB * side, COL_GROUP * side), jnp.float32),
            pltpu.VMEM((products, side, side), jnp.bfloat16),
            pltpu.SemaphoreType.DMA((2,)),
            pltpu.SemaphoreType.DMA((2,)),
            pltpu.SemaphoreType.DMA((1,)),
        ],
        compiler_params=pltpu.CompilerParams(vmem_limit_bytes=60 * 1024 * 1024),
        cost_estimate=pl.CostEstimate(
            flops=flops, bytes_accessed=tile_bytes + partial_bytes + slots * side * side * 2, transcendentals=0
        ),
    )(slot_of, left_index, left_next, columns, partial, outgoing)
    outgoing = outgoing.reshape(devices_all, capacity, side, side)
    received = lax.all_to_all(outgoing, ("row", "col"), split_axis=0, concat_axis=0, tiled=True)
    chunk = devices_all // COPY_STEPS
    block = pl.BlockSpec((chunk, capacity, side, side), lambda i: (i, 0, 0, 0))
    received = pl.pallas_call(
        pass_through,
        out_shape=jax.ShapeDtypeStruct(received.shape, received.dtype),
        grid=(COPY_STEPS,),
        in_specs=[block],
        out_specs=block,
        cost_estimate=pl.CostEstimate(flops=0, bytes_accessed=2 * received.size * 2, transcendentals=0),
    )(received)
    return received[None]


def solution(mesh):
    placed = (
        P("row", "col", None, None, None),
        P(),
        P("row", "col", None, None, None),
        P(),
        P(("row", "col"), None),
    )
    return jax.shard_map(
        body,
        mesh=mesh,
        in_specs=placed,
        out_specs=P(("row", "col"), None, None, None, None),
        check_vma=False,
    )
```

```python
import functools

import jax
import jax.numpy as jnp
from jax import lax
from jax.experimental import pallas as pl
from jax.experimental.pallas import tpu as pltpu
from jax.sharding import PartitionSpec as P

ROWB = 8
KBLK = 16
COLB = 16
COL_GROUP = 4
ROW_GROUP = 8
COPY_STEPS = 2


def from_behind(block, axis, distance):
    devices = range(lax.axis_size(axis))
    route = [((i - distance) % len(devices), i) for i in devices]
    return lax.ppermute(block, axis, route)


def fill(ref, count, value):
    def step(i, carry):
        ref[i] = value
        return carry

    lax.fori_loop(0, count, step, 0)


def invert_places(places, tile, index_ref, positions, stored):
    fill(index_ref, positions, -1)

    def step(n, carry):
        index_ref[places[tile[0], tile[1], n]] = n
        return carry

    lax.fori_loop(0, stored, step, 0)


def multiply_tiles(
    left_tile, right_tile, left_index, right_index, left_dense, right_column, emit, before=None,
    left_ready=None, right_ready=None, column_of=None,
):
    side = left_tile.shape[-1]
    zero_block = jnp.zeros((side, side), left_tile.dtype)
    if left_ready is not None:
        left_ready()

    def densify_left(r, carry):
        rows = pl.ds(pl.multiple_of(r * side, side), side)
        for k in range(KBLK):
            index = left_index[r * KBLK + k]
            block = left_tile[jnp.maximum(index, 0)]
            left_dense[rows, k * side:(k + 1) * side] = jnp.where(index >= 0, block, zero_block)
        return carry

    lax.fori_loop(0, ROWB, densify_left, 0)
    if right_ready is not None:
        right_ready()

    def place_column(cp, clear):
        if clear:
            return
        for k in range(KBLK):
            for cc in range(COL_GROUP):
                index = right_index[k * COLB + cp * COL_GROUP + cc]
                block = right_tile[jnp.maximum(index, 0)]
                right_column[k * side:(k + 1) * side, cc * side:(cc + 1) * side] = jnp.where(
                    index >= 0, block, zero_block
                )

    def column_pair(cp, carry):
        if before is not None:
            before(cp)
        if column_of is None:
            place_column(cp, False)
            column = right_column
        else:
            column = column_of(cp)

        def row_pair(rp, inner):
            rows = pl.ds(pl.multiple_of(rp * ROW_GROUP * side, ROW_GROUP * side), ROW_GROUP * side)
            result = jnp.dot(left_dense[rows, :], column[...], preferred_element_type=jnp.float32)
            emit(rp, cp, rows, result)
            return inner

        lax.fori_loop(0, ROWB // ROW_GROUP, row_pair, 0)
        if column_of is None:
            place_column(cp, True)
        return carry

    lax.fori_loop(0, COLB // COL_GROUP, column_pair, 0)


def first_kernel(
    rows_grid, cols_grid, capacity,
    left_places, right_places, owners, left_tile, right_tile,
    partial, slot_of, left_index_next, right_index_next, outgoing,
    left_dense, right_column, left_index, right_index, counts, filled, zero_ref, zero_sems,
):
    side = left_tile.shape[-1]
    stored = left_tile.shape[0]
    row_here = lax.axis_index("row")
    col_here = lax.axis_index("col")
    row_next = lax.rem(row_here + 1, rows_grid)
    col_next = lax.rem(col_here + 1, cols_grid)
    invert_places(left_places, (row_here, col_here), left_index, ROWB * KBLK, stored)
    invert_places(right_places, (row_here, col_here), right_index, KBLK * COLB, stored)
    invert_places(left_places, (row_here, col_next), left_index_next, ROWB * KBLK, stored)
    invert_places(right_places, (row_next, col_here), right_index_next, KBLK * COLB, stored)
    fill(filled, filled.shape[0], 0)
    fill(counts, counts.shape[0], 0)

    def assign(m, carry):
        owner = owners[m]
        taken = counts[owner]
        slot = owner * capacity + taken
        slot_of[m] = slot
        filled[slot] = 1
        counts[owner] = taken + 1
        return carry

    lax.fori_loop(0, ROWB * COLB, assign, 0)
    zero_ref[...] = jnp.zeros(zero_ref.shape, zero_ref.dtype)

    def zero_slot(s, carry):
        @pl.when(filled[s] == 0)
        def _():
            pltpu.make_async_copy(zero_ref, outgoing.at[s], zero_sems.at[0]).start()

        return carry

    lax.fori_loop(0, outgoing.shape[0], zero_slot, 0)

    def emit(rp, cp, rows, result):
        partial[cp, rows, :] = result

    multiply_tiles(left_tile, right_tile, left_index, right_index, left_dense, right_column, emit)

    unfilled = outgoing.shape[0] - ROWB * COLB
    pltpu.make_async_copy(outgoing.at[pl.ds(0, unfilled)], outgoing.at[pl.ds(0, unfilled)], zero_sems.at[0]).wait()


def column_kernel(right_index, right_tile, columns, column_buf, sems):
    side = right_tile.shape[-1]
    pairs = COLB // COL_GROUP
    zero_block = jnp.zeros((side, side), right_tile.dtype)

    def send(cp, buffer):
        return pltpu.make_async_copy(column_buf.at[buffer], columns.at[cp], sems.at[buffer])

    def column_pair(cp, carry):
        buffer = lax.rem(cp, 2)

        @pl.when(cp >= 2)
        def _():
            send(cp - 2, buffer).wait()

        for k in range(KBLK):
            for cc in range(COL_GROUP):
                index = right_index[k * COLB + cp * COL_GROUP + cc]
                block = right_tile[jnp.maximum(index, 0)]
                column_buf[buffer, k * side:(k + 1) * side, cc * side:(cc + 1) * side] = jnp.where(
                    index >= 0, block, zero_block
                )
        send(cp, buffer).start()
        return carry

    lax.fori_loop(0, pairs, column_pair, 0)
    send(pairs - 2, 0).wait()
    send(pairs - 1, 1).wait()


def second_kernel(
    slot_of, left_index, left_tile, columns, partial, outgoing,
    out,
    left_dense, column_buf, partial_buf, staging, partial_sems, column_sems, out_sems,
):
    side = left_tile.shape[-1]
    pairs = COLB // COL_GROUP
    products = ROWB * COLB

    def partial_copy(cp, buffer):
        return pltpu.make_async_copy(partial.at[cp], partial_buf.at[buffer], partial_sems.at[buffer])

    def column_copy(cp, buffer):
        return pltpu.make_async_copy(columns.at[cp], column_buf.at[buffer], column_sems.at[buffer])

    partial_copy(0, 0).start()
    column_copy(0, 0).start()

    def send_pair(cp):
        for r in range(ROWB):
            for cc in range(COL_GROUP):
                m = r * COLB + cp * COL_GROUP + cc
                pltpu.make_async_copy(staging.at[m], out.at[slot_of[m]], out_sems.at[0]).start()

    def before(cp):
        buffer = lax.rem(cp, 2)

        @pl.when(cp + 1 < pairs)
        def _():
            partial_copy(cp + 1, 1 - buffer).start()
            column_copy(cp + 1, 1 - buffer).start()

        @pl.when(cp > 0)
        def _():
            send_pair(cp - 1)

        partial_copy(cp, buffer).wait()
        column_copy(cp, buffer).wait()

    def emit(rp, cp, rows, result):
        buffer = lax.rem(cp, 2)
        total = result + partial_buf[buffer, rows, :]
        for rr in range(ROW_GROUP):
            for cc in range(COL_GROUP):
                m = (rp * ROW_GROUP + rr) * COLB + cp * COL_GROUP + cc
                piece = total[rr * side:(rr + 1) * side, cc * side:(cc + 1) * side]
                staging[m] = piece.astype(staging.dtype)

    multiply_tiles(
        left_tile, None, left_index, None, left_dense, None, emit, before,
        column_of=lambda cp: column_buf.at[lax.rem(cp, 2)],
    )
    send_pair(pairs - 1)

    pltpu.make_async_copy(staging, out.at[pl.ds(0, products)], out_sems.at[0]).wait()


def pass_through(source, target):
    target[...] = source[...]


def body(left_values, left_places, right_values, right_places, owners):
    rows_grid = lax.axis_size("row")
    cols_grid = lax.axis_size("col")
    devices_all = rows_grid * cols_grid
    left_here = left_values[0, 0]
    right_here = right_values[0, 0]
    side = left_here.shape[-1]
    left_next = lax.optimization_barrier(from_behind(left_here, "col", -1))
    right_next = from_behind(right_here, "row", -1)
    capacity = 2 * ROWB * COLB // devices_all
    slots = devices_all * capacity
    products = ROWB * COLB
    pairs = COLB // COL_GROUP
    smem = pl.BlockSpec(memory_space=pltpu.SMEM)
    vmem = pl.BlockSpec(memory_space=pltpu.VMEM)
    anywhere = pl.BlockSpec(memory_space=pl.ANY)
    work = [
        pltpu.VMEM((ROWB * side, KBLK * side), jnp.bfloat16),
        pltpu.VMEM((KBLK * side, COL_GROUP * side), jnp.bfloat16),
    ]
    flops = 2 * (ROWB * side) * (KBLK * side) * (COLB * side)
    tile_bytes = 2 * left_here.size * 2
    partial_bytes = ROWB * COLB * side * side * 4
    partial, slot_of, left_index, right_index, outgoing = pl.pallas_call(
        functools.partial(first_kernel, rows_grid, cols_grid, capacity),
        out_shape=(
            jax.ShapeDtypeStruct((pairs, ROWB * side, COL_GROUP * side), jnp.float32),
            jax.ShapeDtypeStruct((products,), jnp.int32),
            jax.ShapeDtypeStruct((ROWB * KBLK,), jnp.int32),
            jax.ShapeDtypeStruct((KBLK * COLB,), jnp.int32),
            jax.ShapeDtypeStruct((slots, side, side), jnp.bfloat16),
        ),
        in_specs=[smem, smem, smem, vmem, vmem],
        out_specs=(vmem, smem, smem, smem, anywhere),
        scratch_shapes=work + [
            pltpu.SMEM((ROWB * KBLK,), jnp.int32),
            pltpu.SMEM((KBLK * COLB,), jnp.int32),
            pltpu.SMEM((devices_all,), jnp.int32),
            pltpu.SMEM((slots,), jnp.int32),
            pltpu.VMEM((side, side), jnp.bfloat16),
            pltpu.SemaphoreType.DMA((1,)),
        ],
        compiler_params=pltpu.CompilerParams(vmem_limit_bytes=60 * 1024 * 1024),
        cost_estimate=pl.CostEstimate(flops=flops, bytes_accessed=tile_bytes + partial_bytes, transcendentals=0),
    )(left_places, right_places, owners[0], left_here, right_here)
    column_bytes = pairs * KBLK * side * COL_GROUP * side * 2
    columns = pl.pallas_call(
        column_kernel,
        out_shape=jax.ShapeDtypeStruct((pairs, KBLK * side, COL_GROUP * side), jnp.bfloat16),
        in_specs=[smem, vmem],
        out_specs=anywhere,
        scratch_shapes=[
            pltpu.VMEM((2, KBLK * side, COL_GROUP * side), jnp.bfloat16),
            pltpu.SemaphoreType.DMA((2,)),
        ],
        cost_estimate=pl.CostEstimate(flops=0, bytes_accessed=left_here.size * 2 + column_bytes, transcendentals=0),
    )(right_index, right_next)
    outgoing = pl.pallas_call(
        second_kernel,
        out_shape=jax.ShapeDtypeStruct((slots, side, side), jnp.bfloat16),
        in_specs=[smem, smem, vmem, anywhere, anywhere, anywhere],
        out_specs=anywhere,
        input_output_aliases={5: 0},
        scratch_shapes=[
            pltpu.VMEM((ROWB * side, KBLK * side), jnp.bfloat16),
            pltpu.VMEM((2, KBLK * side, COL_GROUP * side), jnp.bfloat16),
            pltpu.VMEM((2, ROWB * side, COL_GROUP * side), jnp.float32),
            pltpu.VMEM((products, side, side), jnp.bfloat16),
            pltpu.SemaphoreType.DMA((2,)),
            pltpu.SemaphoreType.DMA((2,)),
            pltpu.SemaphoreType.DMA((1,)),
        ],
        compiler_params=pltpu.CompilerParams(vmem_limit_bytes=60 * 1024 * 1024),
        cost_estimate=pl.CostEstimate(
            flops=flops, bytes_accessed=tile_bytes + partial_bytes + slots * side * side * 2, transcendentals=0
        ),
    )(slot_of, left_index, left_next, columns, partial, outgoing)
    outgoing = outgoing.reshape(devices_all, capacity, side, side)
    received = lax.all_to_all(outgoing, ("row", "col"), split_axis=0, concat_axis=0, tiled=True)
    chunk = devices_all // COPY_STEPS
    block = pl.BlockSpec((chunk, capacity, side, side), lambda i: (i, 0, 0, 0))
    received = pl.pallas_call(
        pass_through,
        out_shape=jax.ShapeDtypeStruct(received.shape, received.dtype),
        grid=(COPY_STEPS,),
        in_specs=[block],
        out_specs=block,
        cost_estimate=pl.CostEstimate(flops=0, bytes_accessed=2 * received.size * 2, transcendentals=0),
    )(received)
    return received[None]


def solution(mesh):
    placed = (
        P("row", "col", None, None, None),
        P(),
        P("row", "col", None, None, None),
        P(),
        P(("row", "col"), None),
    )
    return jax.shard_map(
        body,
        mesh=mesh,
        in_specs=placed,
        out_specs=P(("row", "col"), None, None, None, None),
        check_vma=False,
    )
```
